768 devices in a mesh: fsdp: 192 (over y_lo, x, z, core), sp: 4 (over y_hi).
Axes of the slice: x: 4, y: 8 (y_hi: 4, y_lo: 2; y = y_hi * 2 + y_lo), z: 12, core: 2. Of those that a mesh axis runs over, the one named last changes fastest.
Arguments:
- hidden_rows: bfloat16 [98304, 8192], P('fsdp'), may hold values from -6 to 6
- queries: bfloat16 [98304, 4096], P(('fsdp', 'sp')), may hold values from -12 to 12
- key_weight: bfloat16 [8256, 512], P('fsdp', 'sp'), may hold values from -0.0625 to 0.0625
- value_weight: bfloat16 [8256, 512], P('fsdp', 'sp'), may hold values from -0.0625 to 0.0625
- cache_keys: bfloat16 [192, 256, 512], P('fsdp', None, 'sp'), may hold values from -10 to 10
- cache_values: bfloat16 [192, 256, 512], P('fsdp', None, 'sp'), may hold values from -6 to 6
- span_index: int32 [192], P('fsdp'), may hold values from 1 to 255
- prefix_len: int32 [192], P('fsdp'), may hold values from 2 to 256, as said below
Outputs:
- attended: bfloat16 [98304, 4096], P(('fsdp', 'sp'))
The draws below stay inside these ranges and needn't reach their ends.
Inputs may be any that keep to these rules, and one draw needn't show every extreme that they name: `prefix_len`: some group has exactly 256 live slots.
All inputs are finite; a program needn't handle non-finite values.
Results may differ from the reference program's by a relative error of at most 0.014.
Values may be sent and summed in bfloat16 or wider, within the bound.
No kernel may reach another device: no remote copies, remote signals or barrier semaphores. Data moves between devices by JAX's collectives and lax.ppermute only.
A program may use at most 64 MiB of HBM per device.

```python
import math
import jax
import jax.numpy as jnp
from jax import lax

D = 8192
HD = 128
HQ = 32
KVH = 4
YARN_SCALE = 16
ORIG_CTX = 8192
SEQ_LEN = 131072
SPAN = 512
PREF = 256
GROUPS = 192
TOKENS = 98304
D_PAD = 8256
N_FSDP = 192


def draw_queries(key, part):
    keys_split = jax.random.split(jax.random.fold_in(key, 11), 1)
    width = HQ * HD
    values = 1.25 * jnp.clip(jax.random.normal(keys_split[0], (TOKENS, width), jnp.float32), -6.0, 6.0)
    return values.astype(jnp.bfloat16)


def draw_cache_keys(key, part):
    keys_split = jax.random.split(jax.random.fold_in(key, 23), 1)
    width = KVH * HD
    values = jnp.clip(jax.random.normal(keys_split[0], (GROUPS, PREF, width), jnp.float32), -6.0, 6.0)
    return values.astype(jnp.bfloat16)


def draw_prefix_len(key, part):
    keys_split = jax.random.split(jax.random.fold_in(key, 37), 2)
    lengths = jax.random.randint(keys_split[0], (GROUPS,), 2, PREF + 1, dtype=jnp.int32)
    chosen = jax.random.randint(keys_split[1], (), 0, GROUPS, dtype=jnp.int32)
    return lengths.at[chosen].set(PREF)


def set_ends(entries, rng, smallest, largest):
    index_at = [jax.random.randint(jax.random.fold_in(rng, axis), (), 0, length) for axis, length in enumerate(entries.shape)]
    longest = entries.shape.index(max(entries.shape))
    beside = index_at[:longest] + [(index_at[longest] + 1) % entries.shape[longest]] + index_at[longest + 1:]
    return entries.at[tuple(index_at)].set(smallest).at[tuple(beside)].set(largest)


def shard_levels(stream_key, extent, pieces, smallest, largest):
    level = 1.0
    for position, parts in pieces:
        heights = jax.random.uniform(jax.random.fold_in(jax.random.fold_in(stream_key, 6), position), (parts,), jnp.float32, smallest / len(pieces), largest / len(pieces))
        level = level * jnp.repeat(jnp.exp(heights), extent[position] // parts).reshape((-1,) + (1,) * (len(extent) - 1 - position))
    return level


def normal_values(key, shape, spread, most, shards=(), kind=jnp.bfloat16):
    drawn = jax.random.normal(key, shape, jnp.float32) * spread
    if len(shards) > 0:
        drawn = shard_levels(key, shape, shards, -0.22, 0.18) * drawn
    return jnp.clip(drawn, min=-most, max=most).astype(kind)


def setup_inputs(seed: int = 0) -> dict:
    streams_of = jax.random.split(jax.random.key(seed), 9)
    hidden_rows = normal_values(streams_of[0], (TOKENS, D), 1.0, 6.0, ((0, 192),))
    queries = draw_queries(jax.random.fold_in(streams_of[8], 71), 0)
    key_weight = normal_values(streams_of[2], (D_PAD, KVH * HD), D ** -0.5, 0.0625, ((0, 192), (1, 4)))
    value_weight = normal_values(streams_of[3], (D_PAD, KVH * HD), D ** -0.5, 0.0625, ((0, 192), (1, 4)))
    cache_keys = draw_cache_keys(jax.random.fold_in(streams_of[8], 71), 0)
    cache_values = normal_values(streams_of[5], (GROUPS, PREF, KVH * HD), 1.0, 6.0, ((0, 192), (2, 4)))
    span_index = set_ends(jax.random.randint(streams_of[6], (GROUPS,), PREF // SPAN + 1, SEQ_LEN // SPAN), jax.random.fold_in(streams_of[6], 1), PREF // SPAN + 1, (SEQ_LEN // SPAN) - 1).astype(jnp.int32)
    prefix_len = draw_prefix_len(jax.random.fold_in(streams_of[8], 71), 0)
    return dict(hidden_rows=hidden_rows, queries=queries, key_weight=key_weight, value_weight=value_weight, cache_keys=cache_keys, cache_values=cache_values, span_index=span_index, prefix_len=prefix_len)


rope_base = 500000.0
beta_fast = 32.0
beta_slow = 1.0


def yarn_tables(positions, head_size):
    half_size = head_size // 2
    index_row = jnp.arange(half_size, dtype=jnp.float32)
    inverse = jnp.power(rope_base, -2.0 * index_row / head_size)
    wavelength = 2.0 * math.pi / inverse
    ratio = ORIG_CTX / wavelength
    ramp = jnp.clip((ratio - beta_slow) / (beta_fast - beta_slow), 0.0, 1.0)
    freq = inverse / YARN_SCALE * (1.0 - ramp) + inverse * ramp
    factor = 0.1 * math.log(YARN_SCALE) + 1.0
    angles = positions[:, None] * freq[None, :]
    return jnp.cos(angles) * factor, jnp.sin(angles) * factor


def rotate(values, cosine_table, sine_table, head_count):
    row_count = values.shape[0]
    half_size = cosine_table.shape[1]
    split = values.reshape(row_count, head_count, 2, half_size)
    first_half = split[:, :, 0]
    second_half = split[:, :, 1]
    cos_part = cosine_table[:, None, :]
    sin_part = sine_table[:, None, :]
    joined = jnp.stack([first_half * cos_part - second_half * sin_part, second_half * cos_part + first_half * sin_part], axis=2)
    return joined.reshape(row_count, head_count * 2 * half_size)


def reference(hidden_rows, queries, key_weight, value_weight, cache_keys, cache_values, span_index, prefix_len):
    key_rows = key_weight[:D]
    value_rows = value_weight[:D]
    group_size = HQ // KVH
    key_count = PREF + SPAN
    rows_grouped = hidden_rows.reshape(N_FSDP, SPAN, D)
    query_grouped = queries.reshape(N_FSDP, SPAN, HQ * HD)

    def one_group(inputs):
        block_rows, block_queries, old_keys, old_values, block_number, live_count = inputs
        positions = (block_number * SPAN + jnp.arange(SPAN, dtype=jnp.int32)).astype(jnp.float32)
        cosine_table, sine_table = yarn_tables(positions, HD)
        key_sum = jnp.dot(block_rows, key_rows, preferred_element_type=jnp.float32)
        new_keys = rotate(key_sum, cosine_table, sine_table, KVH).astype(jnp.bfloat16)
        new_values = jnp.dot(block_rows, value_rows, preferred_element_type=jnp.float32).astype(jnp.bfloat16)
        rotated_q = rotate(block_queries.astype(jnp.float32), cosine_table, sine_table, HQ).astype(jnp.bfloat16)
        all_keys = jnp.concatenate([old_keys, new_keys], axis=0)
        all_values = jnp.concatenate([old_values, new_values], axis=0)
        slot_index = jnp.arange(key_count, dtype=jnp.int32)
        query_index = jnp.arange(SPAN, dtype=jnp.int32)
        visible = (slot_index[None, :] >= PREF - live_count) & (slot_index[None, :] - PREF <= query_index[:, None])
        query_heads = rotated_q.reshape(SPAN, KVH, group_size, HD).astype(jnp.float32)
        key_heads = all_keys.reshape(key_count, KVH, HD).astype(jnp.float32)
        value_heads = all_values.reshape(key_count, KVH, HD).astype(jnp.float32)
        scores = jnp.einsum("qhgd,khd->hgqk", query_heads, key_heads) * (HD ** -0.5)
        scores = jnp.where(visible, scores, -1e30)
        row_max = jnp.max(scores, axis=-1, keepdims=True)
        weights = jnp.where(visible, jnp.exp(scores - row_max), 0.0)
        total = jnp.sum(weights, axis=-1)
        rounded_weights = weights.astype(jnp.bfloat16)
        summed = jnp.einsum("hgqk,khd->hgqd", rounded_weights.astype(jnp.float32), value_heads)
        result = summed / total[..., None]
        return result.transpose(2, 0, 1, 3).reshape(SPAN, HQ * HD).astype(jnp.bfloat16)

    outputs = lax.map(one_group, (rows_grouped, query_grouped, cache_keys, cache_values, span_index, prefix_len))
    return outputs.reshape(TOKENS, HQ * HD)
```

```python
import math

import jax
import jax.numpy as jnp
from jax import lax
from jax.sharding import PartitionSpec as P

HD = 128
HQ = 32
KVH = 4
YARN_SCALE = 16
ORIG_CTX = 8192


rope_base = 500000.0
beta_fast = 32.0
beta_slow = 1.0


def yarn_tables(positions, head_size):
    half_size = head_size // 2
    index_row = jnp.arange(half_size, dtype=jnp.float32)
    inverse = jnp.power(rope_base, -2.0 * index_row / head_size)
    wavelength = 2.0 * math.pi / inverse
    ratio = ORIG_CTX / wavelength
    ramp = jnp.clip((ratio - beta_slow) / (beta_fast - beta_slow), 0.0, 1.0)
    freq = inverse / YARN_SCALE * (1.0 - ramp) + inverse * ramp
    factor = 0.1 * math.log(YARN_SCALE) + 1.0
    angles = positions[:, None] * freq[None, :]
    return (jnp.cos(angles) * factor, jnp.sin(angles) * factor)


def rotate(values, cosine_table, sine_table, head_count):
    row_count = values.shape[0]
    half_size = cosine_table.shape[1]
    split = values.reshape(row_count, head_count, 2, half_size)
    first_half = split[:, :, 0]
    second_half = split[:, :, 1]
    cos_part = cosine_table[:, None, :]
    sin_part = sine_table[:, None, :]
    joined = jnp.stack(
        [
            first_half * cos_part - second_half * sin_part,
            second_half * cos_part + first_half * sin_part,
        ],
        axis=2,
    )
    return joined.reshape(row_count, head_count * 2 * half_size)


def attend_block(state, query_heads, key_block, value_block, visible):
    running_max, running_sum, weighted = state
    block_len = key_block.shape[0]
    kv_heads = query_heads.shape[0]
    key_heads = key_block.reshape(block_len, kv_heads, HD)
    value_heads = value_block.reshape(block_len, kv_heads, HD)
    scores = jnp.einsum(
        "hgqd,khd->hgqk", query_heads, key_heads, preferred_element_type=jnp.float32
    ) * HD ** (-0.5)
    scores = jnp.where(visible, scores, -1e30)
    new_max = jnp.maximum(running_max, jnp.max(scores, axis=-1))
    rescale = jnp.exp(running_max - new_max)
    weights = jnp.where(visible, jnp.exp(scores - new_max[..., None]), 0.0)
    running_sum = running_sum * rescale + jnp.sum(weights, axis=-1)
    product = jnp.einsum(
        "hgqk,khd->hgqd",
        weights.astype(jnp.bfloat16),
        value_heads,
        preferred_element_type=jnp.float32,
    )
    weighted = weighted * rescale[..., None] + product
    return (new_max, running_sum, weighted)


def attend_all(query_heads, old_keys, old_values, new_keys, new_values, live_count):
    kv_heads, group_size, query_rows, head_size = query_heads.shape
    slot_total = old_keys.shape[0]
    span_rows = new_keys.shape[0]
    state = (
        jnp.full((kv_heads, group_size, query_rows), -1e30, jnp.float32),
        jnp.zeros((kv_heads, group_size, query_rows), jnp.float32),
        jnp.zeros((kv_heads, group_size, query_rows, head_size), jnp.float32),
    )
    cache_block = min(256, slot_total)

    def cache_step(block_number, carried):
        start = block_number * cache_block
        slot_index = start + jnp.arange(cache_block, dtype=jnp.int32)
        visible = (slot_index >= slot_total - live_count)[None, None, None, :]
        return attend_block(carried, query_heads, old_keys, old_values, visible)

    state = lax.fori_loop(0, slot_total // cache_block, cache_step, state)
    new_block = min(256, span_rows)
    query_index = jnp.arange(query_rows, dtype=jnp.int32)

    def new_step(block_number, carried):
        start = block_number * new_block
        key_block = lax.dynamic_slice_in_dim(new_keys, start, new_block, 0)
        value_block = lax.dynamic_slice_in_dim(new_values, start, new_block, 0)
        key_index = start + jnp.arange(new_block, dtype=jnp.int32)
        visible = (key_index[None, :] <= query_index[:, None])[None, None, :, :]
        return attend_block(carried, query_heads, key_block, value_block, visible)

    state = lax.fori_loop(0, span_rows // new_block, new_step, state)
    running_max, running_sum, weighted = state
    result = (weighted / running_sum[..., None]).astype(jnp.bfloat16)
    return result.transpose(2, 0, 1, 3).reshape(query_rows, kv_heads * group_size * head_size)


FSDP_PARTS = (("ylo", 2), ("x", 4), ("z", 12), ("core", 2))
FSDP_AXES = tuple(name for name, _ in FSDP_PARTS)
GATHER_STAGES = (("ylo",), ("x",), ("z",), ("core",))


def gather_weights(shard):
    gathered = shard
    for stage in GATHER_STAGES:
        gathered = lax.all_gather(gathered, stage, axis=0, tiled=False)
        if len(stage) > 1:
            sizes = tuple(dict(FSDP_PARTS)[name] for name in stage)
            gathered = gathered.reshape(sizes + gathered.shape[1:])
    layout = []
    for stage in reversed(GATHER_STAGES):
        layout.extend(stage)
    perm = [layout.index(name) for name in FSDP_AXES]
    rank = len(FSDP_AXES)
    gathered = gathered.transpose(perm + [rank, rank + 1])
    return gathered.reshape(-1, shard.shape[1])


def per_device(
    hidden_rows, queries, key_weight, value_weight, cache_keys, cache_values, span_index, prefix_len
):
    sp_count = lax.axis_size("sp")
    span_rows = hidden_rows.shape[0]
    model_width = hidden_rows.shape[1]
    kv_cols = key_weight.shape[1]
    kv_local = kv_cols // HD
    heads_local = HQ // sp_count
    group_size = HQ // KVH
    positions = (span_index[0] * span_rows + jnp.arange(span_rows, dtype=jnp.int32)).astype(
        jnp.float32
    )
    cosine_table, sine_table = yarn_tables(positions, HD)
    live_count = prefix_len[0]
    old_keys = cache_keys[0]
    old_values = cache_values[0]
    full_old_keys, full_old_values = (old_keys, old_values)
    whole_kv = gather_weights(jnp.concatenate([key_weight, value_weight], axis=1))
    kv_sum = jnp.dot(hidden_rows, whole_kv[:model_width], preferred_element_type=jnp.float32)
    key_sum = kv_sum[:, :kv_cols]
    value_sum = kv_sum[:, kv_cols:]
    new_keys = rotate(key_sum, cosine_table, sine_table, kv_local).astype(jnp.bfloat16)
    new_values = value_sum.astype(jnp.bfloat16)
    by_heads = lax.all_to_all(queries, "sp", split_axis=1, concat_axis=0, tiled=True)
    rotated_q = rotate(by_heads.astype(jnp.float32), cosine_table, sine_table, heads_local).astype(
        jnp.bfloat16
    )
    query_heads = rotated_q.reshape(span_rows, kv_local, group_size, HD).transpose(1, 2, 0, 3)
    by_tokens = attend_all(
        query_heads, full_old_keys, full_old_values, new_keys, new_values, live_count
    )
    return lax.all_to_all(by_tokens, "sp", split_axis=0, concat_axis=1, tiled=True)


def solution(mesh):
    sizes = tuple(size for _, size in FSDP_PARTS)
    fine = jax.sharding.Mesh(
        mesh.devices.reshape(sizes + (mesh.shape["sp"],)), FSDP_AXES + ("sp",)
    )
    fsdp = FSDP_AXES
    placed = (
        P(fsdp, None),
        P(fsdp + ("sp",), None),
        P(fsdp, "sp"),
        P(fsdp, "sp"),
        P(fsdp, None, "sp"),
        P(fsdp, None, "sp"),
        P(fsdp),
        P(fsdp),
    )
    return jax.shard_map(
        per_device, mesh=fine, in_specs=placed, out_specs=P(fsdp + ("sp",), None), check_vma=False
    )
```

```python
import math

import jax
import jax.numpy as jnp
from jax import lax
from jax.sharding import PartitionSpec as P

HD = 128
HQ = 32
KVH = 4
YARN_SCALE = 16
ORIG_CTX = 8192


rope_base = 500000.0
beta_fast = 32.0
beta_slow = 1.0


def yarn_tables(positions, head_size):
    half_size = head_size // 2
    index_row = jnp.arange(half_size, dtype=jnp.float32)
    inverse = jnp.power(rope_base, -2.0 * index_row / head_size)
    wavelength = 2.0 * math.pi / inverse
    ratio = ORIG_CTX / wavelength
    ramp = jnp.clip((ratio - beta_slow) / (beta_fast - beta_slow), 0.0, 1.0)
    freq = inverse / YARN_SCALE * (1.0 - ramp) + inverse * ramp
    factor = 0.1 * math.log(YARN_SCALE) + 1.0
    angles = positions[:, None] * freq[None, :]
    return (jnp.cos(angles) * factor, jnp.sin(angles) * factor)


def rotate(values, cosine_table, sine_table, head_count):
    row_count = values.shape[0]
    half_size = cosine_table.shape[1]
    split = values.reshape(row_count, head_count, 2, half_size)
    first_half = split[:, :, 0]
    second_half = split[:, :, 1]
    cos_part = cosine_table[:, None, :]
    sin_part = sine_table[:, None, :]
    joined = jnp.stack(
        [
            first_half * cos_part - second_half * sin_part,
            second_half * cos_part + first_half * sin_part,
        ],
        axis=2,
    )
    return joined.reshape(row_count, head_count * 2 * half_size)


def attend_block(state, query_heads, key_block, value_block, visible):
    running_max, running_sum, weighted = state
    block_len = key_block.shape[0]
    kv_heads = query_heads.shape[0]
    key_heads = key_block.reshape(block_len, kv_heads, HD)
    value_heads = value_block.reshape(block_len, kv_heads, HD)
    scores = jnp.einsum(
        "hgqd,khd->hgqk", query_heads, key_heads, preferred_element_type=jnp.float32
    ) * HD ** (-0.5)
    scores = jnp.where(visible, scores, -1e30)
    new_max = jnp.maximum(running_max, jnp.max(scores, axis=-1))
    rescale = jnp.exp(running_max - new_max)
    weights = jnp.where(visible, jnp.exp(scores - new_max[..., None]), 0.0)
    running_sum = running_sum * rescale + jnp.sum(weights, axis=-1)
    product = jnp.einsum(
        "hgqk,khd->hgqd",
        weights.astype(jnp.bfloat16),
        value_heads,
        preferred_element_type=jnp.float32,
    )
    weighted = weighted * rescale[..., None] + product
    return (new_max, running_sum, weighted)


def attend_all(query_heads, old_keys, old_values, new_keys, new_values, live_count):
    kv_heads, group_size, query_rows, head_size = query_heads.shape
    slot_total = old_keys.shape[0]
    span_rows = new_keys.shape[0]
    state = (
        jnp.full((kv_heads, group_size, query_rows), -1e30, jnp.float32),
        jnp.zeros((kv_heads, group_size, query_rows), jnp.float32),
        jnp.zeros((kv_heads, group_size, query_rows, head_size), jnp.float32),
    )
    cache_block = min(256, slot_total)

    def cache_step(block_number, carried):
        start = block_number * cache_block
        slot_index = start + jnp.arange(cache_block, dtype=jnp.int32)
        visible = (slot_index >= slot_total - live_count)[None, None, None, :]
        return attend_block(carried, query_heads, old_keys, old_values, visible)

    state = lax.fori_loop(0, slot_total // cache_block, cache_step, state)
    new_block = min(256, span_rows)
    query_index = jnp.arange(query_rows, dtype=jnp.int32)

    def new_step(block_number, carried):
        start = block_number * new_block
        key_block = lax.dynamic_slice_in_dim(new_keys, start, new_block, 0)
        value_block = lax.dynamic_slice_in_dim(new_values, start, new_block, 0)
        key_index = start + jnp.arange(new_block, dtype=jnp.int32)
        visible = (key_index[None, :] <= query_index[:, None])[None, None, :, :]
        return attend_block(carried, query_heads, key_block, value_block, visible)

    state = lax.fori_loop(0, span_rows // new_block, new_step, state)
    running_max, running_sum, weighted = state
    result = (weighted / running_sum[..., None]).astype(jnp.bfloat16)
    return result.transpose(2, 0, 1, 3).reshape(query_rows, kv_heads * group_size * head_size)


FSDP_PARTS = (("ylo", 2), ("x", 4), ("z", 12), ("core", 2))
FSDP_AXES = tuple(name for name, _ in FSDP_PARTS)
GATHER_STAGES = (("ylo",), ("x", "z"), ("core",))


def gather_weights(shard):
    gathered = shard
    for stage in GATHER_STAGES:
        gathered = lax.all_gather(gathered, stage, axis=0, tiled=False)
        if len(stage) > 1:
            sizes = tuple(dict(FSDP_PARTS)[name] for name in stage)
            gathered = gathered.reshape(sizes + gathered.shape[1:])
    layout = []
    for stage in reversed(GATHER_STAGES):
        layout.extend(stage)
    perm = [layout.index(name) for name in FSDP_AXES]
    rank = len(FSDP_AXES)
    gathered = gathered.transpose(perm + [rank, rank + 1])
    return gathered.reshape(-1, shard.shape[1])


def per_device(
    hidden_rows, queries, key_weight, value_weight, cache_keys, cache_values, span_index, prefix_len
):
    sp_count = lax.axis_size("sp")
    span_rows = hidden_rows.shape[0]
    model_width = hidden_rows.shape[1]
    kv_cols = key_weight.shape[1]
    kv_local = kv_cols // HD
    heads_local = HQ // sp_count
    group_size = HQ // KVH
    positions = (span_index[0] * span_rows + jnp.arange(span_rows, dtype=jnp.int32)).astype(
        jnp.float32
    )
    cosine_table, sine_table = yarn_tables(positions, HD)
    live_count = prefix_len[0]
    old_keys = cache_keys[0]
    old_values = cache_values[0]
    full_old_keys, full_old_values = (old_keys, old_values)
    whole_kv = gather_weights(jnp.concatenate([key_weight, value_weight], axis=1))
    kv_sum = jnp.dot(hidden_rows, whole_kv[:model_width], preferred_element_type=jnp.float32)
    key_sum = kv_sum[:, :kv_cols]
    value_sum = kv_sum[:, kv_cols:]
    new_keys = rotate(key_sum, cosine_table, sine_table, kv_local).astype(jnp.bfloat16)
    new_values = value_sum.astype(jnp.bfloat16)
    by_heads = lax.all_to_all(queries, "sp", split_axis=1, concat_axis=0, tiled=True)
    rotated_q = rotate(by_heads.astype(jnp.float32), cosine_table, sine_table, heads_local).astype(
        jnp.bfloat16
    )
    query_heads = rotated_q.reshape(span_rows, kv_local, group_size, HD).transpose(1, 2, 0, 3)
    by_tokens = attend_all(
        query_heads, full_old_keys, full_old_values, new_keys, new_values, live_count
    )
    return lax.all_to_all(by_tokens, "sp", split_axis=0, concat_axis=1, tiled=True)


def solution(mesh):
    sizes = tuple(size for _, size in FSDP_PARTS)
    fine = jax.sharding.Mesh(
        mesh.devices.reshape(sizes + (mesh.shape["sp"],)), FSDP_AXES + ("sp",)
    )
    fsdp = FSDP_AXES
    placed = (
        P(fsdp, None),
        P(fsdp + ("sp",), None),
        P(fsdp, "sp"),
        P(fsdp, "sp"),
        P(fsdp, None, "sp"),
        P(fsdp, None, "sp"),
        P(fsdp),
        P(fsdp),
    )
    return jax.shard_map(
        per_device, mesh=fine, in_specs=placed, out_specs=P(fsdp + ("sp",), None), check_vma=False
    )
```

```python
import math

import jax
import jax.numpy as jnp
from jax import lax
from jax.sharding import PartitionSpec as P

HD = 128
HQ = 32
KVH = 4
YARN_SCALE = 16
ORIG_CTX = 8192


rope_base = 500000.0
beta_fast = 32.0
beta_slow = 1.0


def yarn_tables(positions, head_size):
    half_size = head_size // 2
    index_row = jnp.arange(half_size, dtype=jnp.float32)
    inverse = jnp.power(rope_base, -2.0 * index_row / head_size)
    wavelength = 2.0 * math.pi / inverse
    ratio = ORIG_CTX / wavelength
    ramp = jnp.clip((ratio - beta_slow) / (beta_fast - beta_slow), 0.0, 1.0)
    freq = inverse / YARN_SCALE * (1.0 - ramp) + inverse * ramp
    factor = 0.1 * math.log(YARN_SCALE) + 1.0
    angles = positions[:, None] * freq[None, :]
    return (jnp.cos(angles) * factor, jnp.sin(angles) * factor)


def rotate(values, cosine_table, sine_table, head_count):
    row_count = values.shape[0]
    half_size = cosine_table.shape[1]
    split = values.reshape(row_count, head_count, 2, half_size)
    first_half = split[:, :, 0]
    second_half = split[:, :, 1]
    cos_part = cosine_table[:, None, :]
    sin_part = sine_table[:, None, :]
    joined = jnp.stack(
        [
            first_half * cos_part - second_half * sin_part,
            second_half * cos_part + first_half * sin_part,
        ],
        axis=2,
    )
    return joined.reshape(row_count, head_count * 2 * half_size)


def attend_block(state, query_heads, key_block, value_block, visible):
    running_max, running_sum, weighted = state
    block_len = key_block.shape[0]
    kv_heads = query_heads.shape[0]
    key_heads = key_block.reshape(block_len, kv_heads, HD)
    value_heads = value_block.reshape(block_len, kv_heads, HD)
    scores = jnp.einsum(
        "hgqd,khd->hgqk", query_heads, key_heads, preferred_element_type=jnp.float32
    ) * HD ** (-0.5)
    scores = jnp.where(visible, scores, -1e30)
    new_max = jnp.maximum(running_max, jnp.max(scores, axis=-1))
    rescale = jnp.exp(running_max - new_max)
    weights = jnp.where(visible, jnp.exp(scores - new_max[..., None]), 0.0)
    running_sum = running_sum * rescale + jnp.sum(weights, axis=-1)
    product = jnp.einsum(
        "hgqk,khd->hgqd",
        weights.astype(jnp.bfloat16),
        value_heads,
        preferred_element_type=jnp.float32,
    )
    weighted = weighted * rescale[..., None] + product
    return (new_max, running_sum, weighted)


def attend_all(query_heads, old_keys, old_values, new_keys, new_values, live_count):
    kv_heads, group_size, query_rows, head_size = query_heads.shape
    slot_total = old_keys.shape[0]
    span_rows = new_keys.shape[0]
    state = (
        jnp.full((kv_heads, group_size, query_rows), -1e30, jnp.float32),
        jnp.zeros((kv_heads, group_size, query_rows), jnp.float32),
        jnp.zeros((kv_heads, group_size, query_rows, head_size), jnp.float32),
    )
    cache_block = min(256, slot_total)

    def cache_step(block_number, carried):
        start = block_number * cache_block
        slot_index = start + jnp.arange(cache_block, dtype=jnp.int32)
        visible = (slot_index >= slot_total - live_count)[None, None, None, :]
        return attend_block(carried, query_heads, old_keys, old_values, visible)

    state = lax.fori_loop(0, slot_total // cache_block, cache_step, state)
    new_block = min(256, span_rows)
    query_index = jnp.arange(query_rows, dtype=jnp.int32)

    def new_step(block_number, carried):
        start = block_number * new_block
        key_block = lax.dynamic_slice_in_dim(new_keys, start, new_block, 0)
        value_block = lax.dynamic_slice_in_dim(new_values, start, new_block, 0)
        key_index = start + jnp.arange(new_block, dtype=jnp.int32)
        visible = (key_index[None, :] <= query_index[:, None])[None, None, :, :]
        return attend_block(carried, query_heads, key_block, value_block, visible)

    state = lax.fori_loop(0, span_rows // new_block, new_step, state)
    running_max, running_sum, weighted = state
    result = (weighted / running_sum[..., None]).astype(jnp.bfloat16)
    return result.transpose(2, 0, 1, 3).reshape(query_rows, kv_heads * group_size * head_size)


FSDP_PARTS = (("ylo", 2), ("x", 4), ("z", 12), ("core", 2))
FSDP_AXES = tuple(name for name, _ in FSDP_PARTS)
GATHER_STAGES = (("ylo",), ("x",), ("z",), ("core",))


def gather_weights(shard):
    gathered = shard
    for stage in GATHER_STAGES:
        gathered = lax.all_gather(gathered, stage, axis=0, tiled=False)
        if len(stage) > 1:
            sizes = tuple(dict(FSDP_PARTS)[name] for name in stage)
            gathered = gathered.reshape(sizes + gathered.shape[1:])
    layout = []
    for stage in reversed(GATHER_STAGES):
        layout.extend(stage)
    perm = [layout.index(name) for name in FSDP_AXES]
    rank = len(FSDP_AXES)
    gathered = gathered.transpose(perm + [rank, rank + 1])
    return gathered.reshape(-1, shard.shape[1])


def per_device(
    hidden_rows, queries, key_weight, value_weight, cache_keys, cache_values, span_index, prefix_len
):
    span_rows = hidden_rows.shape[0]
    model_width = hidden_rows.shape[1]
    query_rows = queries.shape[0]
    kv_cols = key_weight.shape[1]
    kv_local = kv_cols // HD
    group_size = HQ // KVH
    slot_total = cache_keys.shape[1]
    sp_index = lax.axis_index("sp")
    block_start = span_index[0] * span_rows
    positions = (block_start + jnp.arange(span_rows, dtype=jnp.int32)).astype(jnp.float32)
    cosine_table, sine_table = yarn_tables(positions, HD)
    first_query = sp_index * query_rows
    query_positions = (
        block_start + first_query + jnp.arange(query_rows, dtype=jnp.int32)
    ).astype(jnp.float32)
    query_cosine, query_sine = yarn_tables(query_positions, HD)
    live_count = prefix_len[0]

    cache_kv = jnp.concatenate([cache_keys[0], cache_values[0]], axis=1)
    cache_all = lax.all_gather(cache_kv, "sp", axis=0, tiled=False)

    whole_kv = gather_weights(jnp.concatenate([key_weight, value_weight], axis=1))
    kv_sum = jnp.dot(hidden_rows, whole_kv[:model_width], preferred_element_type=jnp.float32)
    new_keys = rotate(kv_sum[:, :kv_cols], cosine_table, sine_table, kv_local).astype(jnp.bfloat16)
    new_values = kv_sum[:, kv_cols:].astype(jnp.bfloat16)
    new_all = lax.all_gather(
        jnp.concatenate([new_keys, new_values], axis=1), "sp", axis=0, tiled=False
    )

    rotated_q = rotate(queries.astype(jnp.float32), query_cosine, query_sine, HQ).astype(
        jnp.bfloat16
    )
    query_heads = rotated_q.reshape(query_rows, KVH, group_size, HD)
    scale = HD ** (-0.5)
    old_keys = cache_all[:, :, :HD]
    old_values = cache_all[:, :, HD:]
    fresh_keys = new_all[:, :, :HD]
    fresh_values = new_all[:, :, HD:]
    old_scores = jnp.einsum(
        "thgd,hjd->hgtj", query_heads, old_keys, preferred_element_type=jnp.float32
    ) * scale
    new_scores = jnp.einsum(
        "thgd,hud->hgtu", query_heads, fresh_keys, preferred_element_type=jnp.float32
    ) * scale
    slot_index = jnp.arange(slot_total, dtype=jnp.int32)
    old_visible = (slot_index >= slot_total - live_count)[None, None, None, :]
    key_index = jnp.arange(span_rows, dtype=jnp.int32)
    query_index = first_query + jnp.arange(query_rows, dtype=jnp.int32)
    new_visible = (key_index[None, :] <= query_index[:, None])[None, None, :, :]
    old_scores = jnp.where(old_visible, old_scores, -1e30)
    new_scores = jnp.where(new_visible, new_scores, -1e30)
    row_max = jnp.maximum(jnp.max(old_scores, axis=-1), jnp.max(new_scores, axis=-1))[..., None]
    old_weights = jnp.where(old_visible, jnp.exp(old_scores - row_max), 0.0)
    new_weights = jnp.where(new_visible, jnp.exp(new_scores - row_max), 0.0)
    total = jnp.sum(old_weights, axis=-1) + jnp.sum(new_weights, axis=-1)
    summed = jnp.einsum(
        "hgtj,hjd->hgtd",
        old_weights.astype(jnp.bfloat16),
        old_values,
        preferred_element_type=jnp.float32,
    ) + jnp.einsum(
        "hgtu,hud->hgtd",
        new_weights.astype(jnp.bfloat16),
        fresh_values,
        preferred_element_type=jnp.float32,
    )
    result = (summed / total[..., None]).astype(jnp.bfloat16)
    return result.transpose(2, 0, 1, 3).reshape(query_rows, HQ * HD)


def solution(mesh):
    sizes = tuple(size for _, size in FSDP_PARTS)
    fine = jax.sharding.Mesh(
        mesh.devices.reshape(sizes + (mesh.shape["sp"],)), FSDP_AXES + ("sp",)
    )
    fsdp = FSDP_AXES
    placed = (
        P(fsdp, None),
        P(fsdp + ("sp",), None),
        P(fsdp, "sp"),
        P(fsdp, "sp"),
        P(fsdp, None, "sp"),
        P(fsdp, None, "sp"),
        P(fsdp),
        P(fsdp),
    )
    return jax.shard_map(
        per_device, mesh=fine, in_specs=placed, out_specs=P(fsdp + ("sp",), None), check_vma=False
    )
```

```python
import math

import jax
import jax.numpy as jnp
from jax import lax
from jax.sharding import PartitionSpec as P

HD = 128
HQ = 32
KVH = 4
YARN_SCALE = 16
ORIG_CTX = 8192


rope_base = 500000.0
beta_fast = 32.0
beta_slow = 1.0


def yarn_tables(positions, head_size):
    half_size = head_size // 2
    index_row = jnp.arange(half_size, dtype=jnp.float32)
    inverse = jnp.power(rope_base, -2.0 * index_row / head_size)
    wavelength = 2.0 * math.pi / inverse
    ratio = ORIG_CTX / wavelength
    ramp = jnp.clip((ratio - beta_slow) / (beta_fast - beta_slow), 0.0, 1.0)
    freq = inverse / YARN_SCALE * (1.0 - ramp) + inverse * ramp
    factor = 0.1 * math.log(YARN_SCALE) + 1.0
    angles = positions[:, None] * freq[None, :]
    return (jnp.cos(angles) * factor, jnp.sin(angles) * factor)


def rotate(values, cosine_table, sine_table, head_count):
    row_count = values.shape[0]
    half_size = cosine_table.shape[1]
    split = values.reshape(row_count, head_count, 2, half_size)
    first_half = split[:, :, 0]
    second_half = split[:, :, 1]
    cos_part = cosine_table[:, None, :]
    sin_part = sine_table[:, None, :]
    joined = jnp.stack(
        [
            first_half * cos_part - second_half * sin_part,
            second_half * cos_part + first_half * sin_part,
        ],
        axis=2,
    )
    return joined.reshape(row_count, head_count * 2 * half_size)


def attend_block(state, query_heads, key_block, value_block, visible):
    running_max, running_sum, weighted = state
    block_len = key_block.shape[0]
    kv_heads = query_heads.shape[0]
    key_heads = key_block.reshape(block_len, kv_heads, HD)
    value_heads = value_block.reshape(block_len, kv_heads, HD)
    scores = jnp.einsum(
        "hgqd,khd->hgqk", query_heads, key_heads, preferred_element_type=jnp.float32
    ) * HD ** (-0.5)
    scores = jnp.where(visible, scores, -1e30)
    new_max = jnp.maximum(running_max, jnp.max(scores, axis=-1))
    rescale = jnp.exp(running_max - new_max)
    weights = jnp.where(visible, jnp.exp(scores - new_max[..., None]), 0.0)
    running_sum = running_sum * rescale + jnp.sum(weights, axis=-1)
    product = jnp.einsum(
        "hgqk,khd->hgqd",
        weights.astype(jnp.bfloat16),
        value_heads,
        preferred_element_type=jnp.float32,
    )
    weighted = weighted * rescale[..., None] + product
    return (new_max, running_sum, weighted)


def attend_all(query_heads, old_keys, old_values, new_keys, new_values, live_count):
    kv_heads, group_size, query_rows, head_size = query_heads.shape
    slot_total = old_keys.shape[0]
    span_rows = new_keys.shape[0]
    state = (
        jnp.full((kv_heads, group_size, query_rows), -1e30, jnp.float32),
        jnp.zeros((kv_heads, group_size, query_rows), jnp.float32),
        jnp.zeros((kv_heads, group_size, query_rows, head_size), jnp.float32),
    )
    cache_block = min(256, slot_total)

    def cache_step(block_number, carried):
        start = block_number * cache_block
        slot_index = start + jnp.arange(cache_block, dtype=jnp.int32)
        visible = (slot_index >= slot_total - live_count)[None, None, None, :]
        return attend_block(carried, query_heads, old_keys, old_values, visible)

    state = lax.fori_loop(0, slot_total // cache_block, cache_step, state)
    new_block = min(256, span_rows)
    query_index = jnp.arange(query_rows, dtype=jnp.int32)

    def new_step(block_number, carried):
        start = block_number * new_block
        key_block = lax.dynamic_slice_in_dim(new_keys, start, new_block, 0)
        value_block = lax.dynamic_slice_in_dim(new_values, start, new_block, 0)
        key_index = start + jnp.arange(new_block, dtype=jnp.int32)
        visible = (key_index[None, :] <= query_index[:, None])[None, None, :, :]
        return attend_block(carried, query_heads, key_block, value_block, visible)

    state = lax.fori_loop(0, span_rows // new_block, new_step, state)
    running_max, running_sum, weighted = state
    result = (weighted / running_sum[..., None]).astype(jnp.bfloat16)
    return result.transpose(2, 0, 1, 3).reshape(query_rows, kv_heads * group_size * head_size)


FSDP_PARTS = (("ylo", 2), ("x", 4), ("z", 12), ("core", 2))
FSDP_AXES = tuple(name for name, _ in FSDP_PARTS)
GATHER_STAGES = (("ylo",), ("x",), ("z",), ("core",))


def gather_weights(shard):
    gathered = shard
    for stage in GATHER_STAGES:
        gathered = lax.all_gather(gathered, stage, axis=0, tiled=False)
        if len(stage) > 1:
            sizes = tuple(dict(FSDP_PARTS)[name] for name in stage)
            gathered = gathered.reshape(sizes + gathered.shape[1:])
    layout = []
    for stage in reversed(GATHER_STAGES):
        layout.extend(stage)
    perm = [layout.index(name) for name in FSDP_AXES]
    rank = len(FSDP_AXES)
    gathered = gathered.transpose(perm + [rank, rank + 1])
    return gathered.reshape(-1, shard.shape[1])


def gather_sp(block):
    count = lax.axis_size("sp")
    here = lax.axis_index("sp")
    pieces = [block]
    for shift in range(1, count):
        pairs = [(source, (source + shift) % count) for source in range(count)]
        pieces.append(lax.ppermute(block, "sp", perm=pairs))
    stacked = jnp.stack(pieces)
    order = (here - jnp.arange(count, dtype=jnp.int32)) % count
    return jnp.take(stacked, order, axis=0)


def per_device(
    hidden_rows, queries, key_weight, value_weight, cache_keys, cache_values, span_index, prefix_len
):
    span_rows = hidden_rows.shape[0]
    model_width = hidden_rows.shape[1]
    query_rows = queries.shape[0]
    kv_cols = key_weight.shape[1]
    kv_local = kv_cols // HD
    group_size = HQ // KVH
    slot_total = cache_keys.shape[1]
    sp_index = lax.axis_index("sp")
    block_start = span_index[0] * span_rows
    positions = (block_start + jnp.arange(span_rows, dtype=jnp.int32)).astype(jnp.float32)
    cosine_table, sine_table = yarn_tables(positions, HD)
    first_query = sp_index * query_rows
    query_positions = (
        block_start + first_query + jnp.arange(query_rows, dtype=jnp.int32)
    ).astype(jnp.float32)
    query_cosine, query_sine = yarn_tables(query_positions, HD)
    live_count = prefix_len[0]

    cache_kv = jnp.concatenate([cache_keys[0], cache_values[0]], axis=1)
    cache_all = gather_sp(cache_kv)

    whole_kv = gather_weights(jnp.concatenate([key_weight, value_weight], axis=1))
    kv_sum = jnp.dot(hidden_rows, whole_kv[:model_width], preferred_element_type=jnp.float32)
    new_keys = rotate(kv_sum[:, :kv_cols], cosine_table, sine_table, kv_local).astype(jnp.bfloat16)
    new_values = kv_sum[:, kv_cols:].astype(jnp.bfloat16)
    new_all = gather_sp(jnp.concatenate([new_keys, new_values], axis=1))

    rotated_q = rotate(queries.astype(jnp.float32), query_cosine, query_sine, HQ).astype(
        jnp.bfloat16
    )
    query_heads = rotated_q.reshape(query_rows, KVH, group_size, HD)
    scale = HD ** (-0.5)
    old_keys = cache_all[:, :, :HD]
    old_values = cache_all[:, :, HD:]
    fresh_keys = new_all[:, :, :HD]
    fresh_values = new_all[:, :, HD:]
    old_scores = jnp.einsum(
        "thgd,hjd->hgtj", query_heads, old_keys, preferred_element_type=jnp.float32
    ) * scale
    new_scores = jnp.einsum(
        "thgd,hud->hgtu", query_heads, fresh_keys, preferred_element_type=jnp.float32
    ) * scale
    slot_index = jnp.arange(slot_total, dtype=jnp.int32)
    old_visible = (slot_index >= slot_total - live_count)[None, None, None, :]
    key_index = jnp.arange(span_rows, dtype=jnp.int32)
    query_index = first_query + jnp.arange(query_rows, dtype=jnp.int32)
    new_visible = (key_index[None, :] <= query_index[:, None])[None, None, :, :]
    old_scores = jnp.where(old_visible, old_scores, -1e30)
    new_scores = jnp.where(new_visible, new_scores, -1e30)
    row_max = jnp.maximum(jnp.max(old_scores, axis=-1), jnp.max(new_scores, axis=-1))[..., None]
    old_weights = jnp.where(old_visible, jnp.exp(old_scores - row_max), 0.0)
    new_weights = jnp.where(new_visible, jnp.exp(new_scores - row_max), 0.0)
    total = jnp.sum(old_weights, axis=-1) + jnp.sum(new_weights, axis=-1)
    summed = jnp.einsum(
        "hgtj,hjd->hgtd",
        old_weights.astype(jnp.bfloat16),
        old_values,
        preferred_element_type=jnp.float32,
    ) + jnp.einsum(
        "hgtu,hud->hgtd",
        new_weights.astype(jnp.bfloat16),
        fresh_values,
        preferred_element_type=jnp.float32,
    )
    result = (summed / total[..., None]).astype(jnp.bfloat16)
    return result.transpose(2, 0, 1, 3).reshape(query_rows, HQ * HD)


def solution(mesh):
    sizes = tuple(size for _, size in FSDP_PARTS)
    fine = jax.sharding.Mesh(
        mesh.devices.reshape(sizes + (mesh.shape["sp"],)), FSDP_AXES + ("sp",)
    )
    fsdp = FSDP_AXES
    placed = (
        P(fsdp, None),
        P(fsdp + ("sp",), None),
        P(fsdp, "sp"),
        P(fsdp, "sp"),
        P(fsdp, None, "sp"),
        P(fsdp, None, "sp"),
        P(fsdp),
        P(fsdp),
    )
    return jax.shard_map(
        per_device, mesh=fine, in_specs=placed, out_specs=P(fsdp + ("sp",), None), check_vma=False
    )
```

```python
import math

import jax
import jax.numpy as jnp
from jax import lax
from jax.sharding import PartitionSpec as P

HD = 128
HQ = 32
KVH = 4
YARN_SCALE = 16
ORIG_CTX = 8192


rope_base = 500000.0
beta_fast = 32.0
beta_slow = 1.0


def yarn_tables(positions, head_size):
    half_size = head_size // 2
    index_row = jnp.arange(half_size, dtype=jnp.float32)
    inverse = jnp.power(rope_base, -2.0 * index_row / head_size)
    wavelength = 2.0 * math.pi / inverse
    ratio = ORIG_CTX / wavelength
    ramp = jnp.clip((ratio - beta_slow) / (beta_fast - beta_slow), 0.0, 1.0)
    freq = inverse / YARN_SCALE * (1.0 - ramp) + inverse * ramp
    factor = 0.1 * math.log(YARN_SCALE) + 1.0
    angles = positions[:, None] * freq[None, :]
    return (jnp.cos(angles) * factor, jnp.sin(angles) * factor)


def rotate(values, cosine_table, sine_table, head_count):
    row_count = values.shape[0]
    half_size = cosine_table.shape[1]
    split = values.reshape(row_count, head_count, 2, half_size)
    first_half = split[:, :, 0]
    second_half = split[:, :, 1]
    cos_part = cosine_table[:, None, :]
    sin_part = sine_table[:, None, :]
    joined = jnp.stack(
        [
            first_half * cos_part - second_half * sin_part,
            second_half * cos_part + first_half * sin_part,
        ],
        axis=2,
    )
    return joined.reshape(row_count, head_count * 2 * half_size)


def attend_block(state, query_heads, key_block, value_block, visible):
    running_max, running_sum, weighted = state
    block_len = key_block.shape[0]
    kv_heads = query_heads.shape[0]
    key_heads = key_block.reshape(block_len, kv_heads, HD)
    value_heads = value_block.reshape(block_len, kv_heads, HD)
    scores = jnp.einsum(
        "hgqd,khd->hgqk", query_heads, key_heads, preferred_element_type=jnp.float32
    ) * HD ** (-0.5)
    scores = jnp.where(visible, scores, -1e30)
    new_max = jnp.maximum(running_max, jnp.max(scores, axis=-1))
    rescale = jnp.exp(running_max - new_max)
    weights = jnp.where(visible, jnp.exp(scores - new_max[..., None]), 0.0)
    running_sum = running_sum * rescale + jnp.sum(weights, axis=-1)
    product = jnp.einsum(
        "hgqk,khd->hgqd",
        weights.astype(jnp.bfloat16),
        value_heads,
        preferred_element_type=jnp.float32,
    )
    weighted = weighted * rescale[..., None] + product
    return (new_max, running_sum, weighted)


def attend_all(query_heads, old_keys, old_values, new_keys, new_values, live_count):
    kv_heads, group_size, query_rows, head_size = query_heads.shape
    slot_total = old_keys.shape[0]
    span_rows = new_keys.shape[0]
    state = (
        jnp.full((kv_heads, group_size, query_rows), -1e30, jnp.float32),
        jnp.zeros((kv_heads, group_size, query_rows), jnp.float32),
        jnp.zeros((kv_heads, group_size, query_rows, head_size), jnp.float32),
    )
    cache_block = min(256, slot_total)

    def cache_step(block_number, carried):
        start = block_number * cache_block
        slot_index = start + jnp.arange(cache_block, dtype=jnp.int32)
        visible = (slot_index >= slot_total - live_count)[None, None, None, :]
        return attend_block(carried, query_heads, old_keys, old_values, visible)

    state = lax.fori_loop(0, slot_total // cache_block, cache_step, state)
    new_block = min(256, span_rows)
    query_index = jnp.arange(query_rows, dtype=jnp.int32)

    def new_step(block_number, carried):
        start = block_number * new_block
        key_block = lax.dynamic_slice_in_dim(new_keys, start, new_block, 0)
        value_block = lax.dynamic_slice_in_dim(new_values, start, new_block, 0)
        key_index = start + jnp.arange(new_block, dtype=jnp.int32)
        visible = (key_index[None, :] <= query_index[:, None])[None, None, :, :]
        return attend_block(carried, query_heads, key_block, value_block, visible)

    state = lax.fori_loop(0, span_rows // new_block, new_step, state)
    running_max, running_sum, weighted = state
    result = (weighted / running_sum[..., None]).astype(jnp.bfloat16)
    return result.transpose(2, 0, 1, 3).reshape(query_rows, kv_heads * group_size * head_size)


FSDP_PARTS = (("ylo", 2), ("x", 4), ("z", 12), ("core", 2))
FSDP_AXES = tuple(name for name, _ in FSDP_PARTS)
GATHER_STAGES = (("ylo",), ("x",), ("z",), ("core",))


def gather_weights(shard):
    gathered = shard
    for stage in GATHER_STAGES:
        gathered = lax.all_gather(gathered, stage, axis=0, tiled=False)
        if len(stage) > 1:
            sizes = tuple(dict(FSDP_PARTS)[name] for name in stage)
            gathered = gathered.reshape(sizes + gathered.shape[1:])
    return gathered.reshape(-1, shard.shape[1])


def gathered_order_columns(hidden_rows, shard_rows, padded_rows):
    sizes = tuple(size for _, size in FSDP_PARTS)
    devices = math.prod(sizes)
    rows = hidden_rows.shape[0]
    wide = jnp.pad(hidden_rows, ((0, 0), (0, devices * shard_rows - hidden_rows.shape[1])))
    split = wide.reshape((rows,) + sizes + (shard_rows,))
    layout = []
    for stage in reversed(GATHER_STAGES):
        layout.extend(stage)
    perm = [0] + [1 + FSDP_AXES.index(name) for name in layout] + [1 + len(FSDP_AXES)]
    moved = split.transpose(perm)
    moved = jnp.pad(moved, [(0, 0)] * (len(perm) - 1) + [(0, padded_rows - shard_rows)])
    return moved.reshape(rows, -1)


def gather_sp(block):
    count = lax.axis_size("sp")
    here = lax.axis_index("sp")
    pieces = [block]
    for shift in range(1, count):
        pairs = [(source, (source + shift) % count) for source in range(count)]
        pieces.append(lax.ppermute(block, "sp", perm=pairs))
    stacked = jnp.stack(pieces)
    order = (here - jnp.arange(count, dtype=jnp.int32)) % count
    return jnp.take(stacked, order, axis=0)


def per_device(
    hidden_rows, queries, key_weight, value_weight, cache_keys, cache_values, span_index, prefix_len
):
    span_rows = hidden_rows.shape[0]
    model_width = hidden_rows.shape[1]
    query_rows = queries.shape[0]
    kv_cols = key_weight.shape[1]
    kv_local = kv_cols // HD
    group_size = HQ // KVH
    slot_total = cache_keys.shape[1]
    sp_index = lax.axis_index("sp")
    block_start = span_index[0] * span_rows
    positions = (block_start + jnp.arange(span_rows, dtype=jnp.int32)).astype(jnp.float32)
    cosine_table, sine_table = yarn_tables(positions, HD)
    first_query = sp_index * query_rows
    query_positions = (
        block_start + first_query + jnp.arange(query_rows, dtype=jnp.int32)
    ).astype(jnp.float32)
    query_cosine, query_sine = yarn_tables(query_positions, HD)
    live_count = prefix_len[0]

    cache_kv = jnp.concatenate([cache_keys[0], cache_values[0]], axis=1)
    cache_all = gather_sp(cache_kv)

    shard = jnp.concatenate([key_weight, value_weight], axis=1)
    shard_rows = shard.shape[0]
    padded_rows = -(-shard_rows // 16) * 16
    whole_kv = gather_weights(jnp.pad(shard, ((0, padded_rows - shard_rows), (0, 0))))
    ordered_rows = gathered_order_columns(hidden_rows, shard_rows, padded_rows)
    kv_sum = jnp.dot(ordered_rows, whole_kv, preferred_element_type=jnp.float32)
    new_keys = rotate(kv_sum[:, :kv_cols], cosine_table, sine_table, kv_local).astype(jnp.bfloat16)
    new_values = kv_sum[:, kv_cols:].astype(jnp.bfloat16)
    new_all = lax.all_gather(
        jnp.concatenate([new_keys, new_values], axis=1), "sp", axis=0, tiled=False
    )

    rotated_q = rotate(queries.astype(jnp.float32), query_cosine, query_sine, HQ).astype(
        jnp.bfloat16
    )
    query_heads = rotated_q.reshape(query_rows, KVH, group_size, HD)
    scale = HD ** (-0.5)
    old_keys = cache_all[:, :, :HD]
    old_values = cache_all[:, :, HD:]
    fresh_keys = new_all[:, :, :HD]
    fresh_values = new_all[:, :, HD:]
    old_scores = jnp.einsum(
        "thgd,hjd->hgtj", query_heads, old_keys, preferred_element_type=jnp.float32
    ) * scale
    new_scores = jnp.einsum(
        "thgd,hud->hgtu", query_heads, fresh_keys, preferred_element_type=jnp.float32
    ) * scale
    slot_index = jnp.arange(slot_total, dtype=jnp.int32)
    old_visible = (slot_index >= slot_total - live_count)[None, None, None, :]
    key_index = jnp.arange(span_rows, dtype=jnp.int32)
    query_index = first_query + jnp.arange(query_rows, dtype=jnp.int32)
    new_visible = (key_index[None, :] <= query_index[:, None])[None, None, :, :]
    old_scores = jnp.where(old_visible, old_scores, -1e30)
    new_scores = jnp.where(new_visible, new_scores, -1e30)
    row_max = jnp.maximum(jnp.max(old_scores, axis=-1), jnp.max(new_scores, axis=-1))[..., None]
    old_weights = jnp.where(old_visible, jnp.exp(old_scores - row_max), 0.0)
    new_weights = jnp.where(new_visible, jnp.exp(new_scores - row_max), 0.0)
    total = jnp.sum(old_weights, axis=-1) + jnp.sum(new_weights, axis=-1)
    summed = jnp.einsum(
        "hgtj,hjd->hgtd",
        old_weights.astype(jnp.bfloat16),
        old_values,
        preferred_element_type=jnp.float32,
    ) + jnp.einsum(
        "hgtu,hud->hgtd",
        new_weights.astype(jnp.bfloat16),
        fresh_values,
        preferred_element_type=jnp.float32,
    )
    result = (summed / total[..., None]).astype(jnp.bfloat16)
    return result.transpose(2, 0, 1, 3).reshape(query_rows, HQ * HD)


def solution(mesh):
    sizes = tuple(size for _, size in FSDP_PARTS)
    fine = jax.sharding.Mesh(
        mesh.devices.reshape(sizes + (mesh.shape["sp"],)), FSDP_AXES + ("sp",)
    )
    fsdp = FSDP_AXES
    placed = (
        P(fsdp, None),
        P(fsdp + ("sp",), None),
        P(fsdp, "sp"),
        P(fsdp, "sp"),
        P(fsdp, None, "sp"),
        P(fsdp, None, "sp"),
        P(fsdp),
        P(fsdp),
    )
    return jax.shard_map(
        per_device, mesh=fine, in_specs=placed, out_specs=P(fsdp + ("sp",), None), check_vma=False
    )
```

```python
import math

import jax
import jax.numpy as jnp
from jax import lax
from jax.sharding import PartitionSpec as P

HD = 128
HQ = 32
KVH = 4
YARN_SCALE = 16
ORIG_CTX = 8192


rope_base = 500000.0
beta_fast = 32.0
beta_slow = 1.0


def yarn_tables(positions, head_size):
    half_size = head_size // 2
    index_row = jnp.arange(half_size, dtype=jnp.float32)
    inverse = jnp.power(rope_base, -2.0 * index_row / head_size)
    wavelength = 2.0 * math.pi / inverse
    ratio = ORIG_CTX / wavelength
    ramp = jnp.clip((ratio - beta_slow) / (beta_fast - beta_slow), 0.0, 1.0)
    freq = inverse / YARN_SCALE * (1.0 - ramp) + inverse * ramp
    factor = 0.1 * math.log(YARN_SCALE) + 1.0
    angles = positions[:, None] * freq[None, :]
    return (jnp.cos(angles) * factor, jnp.sin(angles) * factor)


def rotate(values, cosine_table, sine_table, head_count):
    row_count = values.shape[0]
    half_size = cosine_table.shape[1]
    split = values.reshape(row_count, head_count, 2, half_size)
    first_half = split[:, :, 0]
    second_half = split[:, :, 1]
    cos_part = cosine_table[:, None, :]
    sin_part = sine_table[:, None, :]
    joined = jnp.stack(
        [
            first_half * cos_part - second_half * sin_part,
            second_half * cos_part + first_half * sin_part,
        ],
        axis=2,
    )
    return joined.reshape(row_count, head_count * 2 * half_size)


def attend_block(state, query_heads, key_block, value_block, visible):
    running_max, running_sum, weighted = state
    block_len = key_block.shape[0]
    kv_heads = query_heads.shape[0]
    key_heads = key_block.reshape(block_len, kv_heads, HD)
    value_heads = value_block.reshape(block_len, kv_heads, HD)
    scores = jnp.einsum(
        "hgqd,khd->hgqk", query_heads, key_heads, preferred_element_type=jnp.float32
    ) * HD ** (-0.5)
    scores = jnp.where(visible, scores, -1e30)
    new_max = jnp.maximum(running_max, jnp.max(scores, axis=-1))
    rescale = jnp.exp(running_max - new_max)
    weights = jnp.where(visible, jnp.exp(scores - new_max[..., None]), 0.0)
    running_sum = running_sum * rescale + jnp.sum(weights, axis=-1)
    product = jnp.einsum(
        "hgqk,khd->hgqd",
        weights.astype(jnp.bfloat16),
        value_heads,
        preferred_element_type=jnp.float32,
    )
    weighted = weighted * rescale[..., None] + product
    return (new_max, running_sum, weighted)


def attend_all(query_heads, old_keys, old_values, new_keys, new_values, live_count):
    kv_heads, group_size, query_rows, head_size = query_heads.shape
    slot_total = old_keys.shape[0]
    span_rows = new_keys.shape[0]
    state = (
        jnp.full((kv_heads, group_size, query_rows), -1e30, jnp.float32),
        jnp.zeros((kv_heads, group_size, query_rows), jnp.float32),
        jnp.zeros((kv_heads, group_size, query_rows, head_size), jnp.float32),
    )
    cache_block = min(256, slot_total)

    def cache_step(block_number, carried):
        start = block_number * cache_block
        slot_index = start + jnp.arange(cache_block, dtype=jnp.int32)
        visible = (slot_index >= slot_total - live_count)[None, None, None, :]
        return attend_block(carried, query_heads, old_keys, old_values, visible)

    state = lax.fori_loop(0, slot_total // cache_block, cache_step, state)
    new_block = min(256, span_rows)
    query_index = jnp.arange(query_rows, dtype=jnp.int32)

    def new_step(block_number, carried):
        start = block_number * new_block
        key_block = lax.dynamic_slice_in_dim(new_keys, start, new_block, 0)
        value_block = lax.dynamic_slice_in_dim(new_values, start, new_block, 0)
        key_index = start + jnp.arange(new_block, dtype=jnp.int32)
        visible = (key_index[None, :] <= query_index[:, None])[None, None, :, :]
        return attend_block(carried, query_heads, key_block, value_block, visible)

    state = lax.fori_loop(0, span_rows // new_block, new_step, state)
    running_max, running_sum, weighted = state
    result = (weighted / running_sum[..., None]).astype(jnp.bfloat16)
    return result.transpose(2, 0, 1, 3).reshape(query_rows, kv_heads * group_size * head_size)


FSDP_PARTS = (("ylo", 2), ("x", 4), ("zhi", 3), ("zlo", 4), ("core", 2))
FSDP_AXES = tuple(name for name, _ in FSDP_PARTS)
GATHER_STAGES = (("ylo",), ("x",), ("zlo",), ("zhi",), ("core",))


def gather_weights(shard):
    gathered = shard
    for stage in GATHER_STAGES:
        gathered = lax.all_gather(gathered, stage, axis=0, tiled=False)
        if len(stage) > 1:
            sizes = tuple(dict(FSDP_PARTS)[name] for name in stage)
            gathered = gathered.reshape(sizes + gathered.shape[1:])
    layout = []
    for stage in reversed(GATHER_STAGES):
        layout.extend(stage)
    perm = [layout.index(name) for name in FSDP_AXES]
    rank = len(FSDP_AXES)
    gathered = gathered.transpose(perm + [rank, rank + 1])
    return gathered.reshape(-1, shard.shape[1])


def gather_sp(block):
    count = lax.axis_size("sp")
    here = lax.axis_index("sp")
    pieces = [block]
    for shift in range(1, count):
        pairs = [(source, (source + shift) % count) for source in range(count)]
        pieces.append(lax.ppermute(block, "sp", perm=pairs))
    stacked = jnp.stack(pieces)
    order = (here - jnp.arange(count, dtype=jnp.int32)) % count
    return jnp.take(stacked, order, axis=0)


def per_device(
    hidden_rows, queries, key_weight, value_weight, cache_keys, cache_values, span_index, prefix_len
):
    span_rows = hidden_rows.shape[0]
    model_width = hidden_rows.shape[1]
    query_rows = queries.shape[0]
    kv_cols = key_weight.shape[1]
    kv_local = kv_cols // HD
    group_size = HQ // KVH
    slot_total = cache_keys.shape[1]
    sp_index = lax.axis_index("sp")
    block_start = span_index[0] * span_rows
    positions = (block_start + jnp.arange(span_rows, dtype=jnp.int32)).astype(jnp.float32)
    cosine_table, sine_table = yarn_tables(positions, HD)
    first_query = sp_index * query_rows
    query_positions = (
        block_start + first_query + jnp.arange(query_rows, dtype=jnp.int32)
    ).astype(jnp.float32)
    query_cosine, query_sine = yarn_tables(query_positions, HD)
    live_count = prefix_len[0]

    cache_kv = jnp.concatenate([cache_keys[0], cache_values[0]], axis=1)
    cache_all = gather_sp(cache_kv)

    whole_kv = gather_weights(jnp.concatenate([key_weight, value_weight], axis=1))
    kv_sum = jnp.dot(hidden_rows, whole_kv[:model_width], preferred_element_type=jnp.float32)
    new_keys = rotate(kv_sum[:, :kv_cols], cosine_table, sine_table, kv_local).astype(jnp.bfloat16)
    new_values = kv_sum[:, kv_cols:].astype(jnp.bfloat16)
    new_all = gather_sp(jnp.concatenate([new_keys, new_values], axis=1))

    rotated_q = rotate(queries.astype(jnp.float32), query_cosine, query_sine, HQ).astype(
        jnp.bfloat16
    )
    query_heads = rotated_q.reshape(query_rows, KVH, group_size, HD)
    scale = HD ** (-0.5)
    old_keys = cache_all[:, :, :HD]
    old_values = cache_all[:, :, HD:]
    fresh_keys = new_all[:, :, :HD]
    fresh_values = new_all[:, :, HD:]
    old_scores = jnp.einsum(
        "thgd,hjd->hgtj", query_heads, old_keys, preferred_element_type=jnp.float32
    ) * scale
    new_scores = jnp.einsum(
        "thgd,hud->hgtu", query_heads, fresh_keys, preferred_element_type=jnp.float32
    ) * scale
    slot_index = jnp.arange(slot_total, dtype=jnp.int32)
    old_visible = (slot_index >= slot_total - live_count)[None, None, None, :]
    key_index = jnp.arange(span_rows, dtype=jnp.int32)
    query_index = first_query + jnp.arange(query_rows, dtype=jnp.int32)
    new_visible = (key_index[None, :] <= query_index[:, None])[None, None, :, :]
    old_scores = jnp.where(old_visible, old_scores, -1e30)
    new_scores = jnp.where(new_visible, new_scores, -1e30)
    row_max = jnp.maximum(jnp.max(old_scores, axis=-1), jnp.max(new_scores, axis=-1))[..., None]
    old_weights = jnp.where(old_visible, jnp.exp(old_scores - row_max), 0.0)
    new_weights = jnp.where(new_visible, jnp.exp(new_scores - row_max), 0.0)
    total = jnp.sum(old_weights, axis=-1) + jnp.sum(new_weights, axis=-1)
    summed = jnp.einsum(
        "hgtj,hjd->hgtd",
        old_weights.astype(jnp.bfloat16),
        old_values,
        preferred_element_type=jnp.float32,
    ) + jnp.einsum(
        "hgtu,hud->hgtd",
        new_weights.astype(jnp.bfloat16),
        fresh_values,
        preferred_element_type=jnp.float32,
    )
    result = (summed / total[..., None]).astype(jnp.bfloat16)
    return result.transpose(2, 0, 1, 3).reshape(query_rows, HQ * HD)


def solution(mesh):
    sizes = tuple(size for _, size in FSDP_PARTS)
    fine = jax.sharding.Mesh(
        mesh.devices.reshape(sizes + (mesh.shape["sp"],)), FSDP_AXES + ("sp",)
    )
    fsdp = FSDP_AXES
    placed = (
        P(fsdp, None),
        P(fsdp + ("sp",), None),
        P(fsdp, "sp"),
        P(fsdp, "sp"),
        P(fsdp, None, "sp"),
        P(fsdp, None, "sp"),
        P(fsdp),
        P(fsdp),
    )
    return jax.shard_map(
        per_device, mesh=fine, in_specs=placed, out_specs=P(fsdp + ("sp",), None), check_vma=False
    )
```

```python
import math

import jax
import jax.numpy as jnp
from jax import lax
from jax.sharding import PartitionSpec as P

HD = 128
HQ = 32
KVH = 4
YARN_SCALE = 16
ORIG_CTX = 8192


rope_base = 500000.0
beta_fast = 32.0
beta_slow = 1.0


def yarn_tables(positions, head_size):
    half_size = head_size // 2
    index_row = jnp.arange(half_size, dtype=jnp.float32)
    inverse = jnp.power(rope_base, -2.0 * index_row / head_size)
    wavelength = 2.0 * math.pi / inverse
    ratio = ORIG_CTX / wavelength
    ramp = jnp.clip((ratio - beta_slow) / (beta_fast - beta_slow), 0.0, 1.0)
    freq = inverse / YARN_SCALE * (1.0 - ramp) + inverse * ramp
    factor = 0.1 * math.log(YARN_SCALE) + 1.0
    angles = positions[:, None] * freq[None, :]
    return (jnp.cos(angles) * factor, jnp.sin(angles) * factor)


def rotate(values, cosine_table, sine_table, head_count):
    row_count = values.shape[0]
    half_size = cosine_table.shape[1]
    split = values.reshape(row_count, head_count, 2, half_size)
    first_half = split[:, :, 0]
    second_half = split[:, :, 1]
    cos_part = cosine_table[:, None, :]
    sin_part = sine_table[:, None, :]
    joined = jnp.stack(
        [
            first_half * cos_part - second_half * sin_part,
            second_half * cos_part + first_half * sin_part,
        ],
        axis=2,
    )
    return joined.reshape(row_count, head_count * 2 * half_size)


def attend_block(state, query_heads, key_block, value_block, visible):
    running_max, running_sum, weighted = state
    block_len = key_block.shape[0]
    kv_heads = query_heads.shape[0]
    key_heads = key_block.reshape(block_len, kv_heads, HD)
    value_heads = value_block.reshape(block_len, kv_heads, HD)
    scores = jnp.einsum(
        "hgqd,khd->hgqk", query_heads, key_heads, preferred_element_type=jnp.float32
    ) * HD ** (-0.5)
    scores = jnp.where(visible, scores, -1e30)
    new_max = jnp.maximum(running_max, jnp.max(scores, axis=-1))
    rescale = jnp.exp(running_max - new_max)
    weights = jnp.where(visible, jnp.exp(scores - new_max[..., None]), 0.0)
    running_sum = running_sum * rescale + jnp.sum(weights, axis=-1)
    product = jnp.einsum(
        "hgqk,khd->hgqd",
        weights.astype(jnp.bfloat16),
        value_heads,
        preferred_element_type=jnp.float32,
    )
    weighted = weighted * rescale[..., None] + product
    return (new_max, running_sum, weighted)


def attend_all(query_heads, old_keys, old_values, new_keys, new_values, live_count):
    kv_heads, group_size, query_rows, head_size = query_heads.shape
    slot_total = old_keys.shape[0]
    span_rows = new_keys.shape[0]
    state = (
        jnp.full((kv_heads, group_size, query_rows), -1e30, jnp.float32),
        jnp.zeros((kv_heads, group_size, query_rows), jnp.float32),
        jnp.zeros((kv_heads, group_size, query_rows, head_size), jnp.float32),
    )
    cache_block = min(256, slot_total)

    def cache_step(block_number, carried):
        start = block_number * cache_block
        slot_index = start + jnp.arange(cache_block, dtype=jnp.int32)
        visible = (slot_index >= slot_total - live_count)[None, None, None, :]
        return attend_block(carried, query_heads, old_keys, old_values, visible)

    state = lax.fori_loop(0, slot_total // cache_block, cache_step, state)
    new_block = min(256, span_rows)
    query_index = jnp.arange(query_rows, dtype=jnp.int32)

    def new_step(block_number, carried):
        start = block_number * new_block
        key_block = lax.dynamic_slice_in_dim(new_keys, start, new_block, 0)
        value_block = lax.dynamic_slice_in_dim(new_values, start, new_block, 0)
        key_index = start + jnp.arange(new_block, dtype=jnp.int32)
        visible = (key_index[None, :] <= query_index[:, None])[None, None, :, :]
        return attend_block(carried, query_heads, key_block, value_block, visible)

    state = lax.fori_loop(0, span_rows // new_block, new_step, state)
    running_max, running_sum, weighted = state
    result = (weighted / running_sum[..., None]).astype(jnp.bfloat16)
    return result.transpose(2, 0, 1, 3).reshape(query_rows, kv_heads * group_size * head_size)


FSDP_PARTS = (("ylo", 2), ("x", 4), ("z", 12), ("core", 2))
FSDP_AXES = tuple(name for name, _ in FSDP_PARTS)
GATHER_STAGES = (("ylo",), ("x",), ("z",))


def gather_weights(shard):
    gathered = shard
    for stage in GATHER_STAGES:
        gathered = lax.all_gather(gathered, stage, axis=0, tiled=False)
    other = lax.ppermute(gathered, "core", perm=[(0, 1), (1, 0)])
    here = lax.axis_index("core")
    order = (jnp.arange(2, dtype=jnp.int32) + here) % 2
    gathered = jnp.take(jnp.stack([gathered, other]), order, axis=0)
    layout = ["core"]
    for stage in reversed(GATHER_STAGES):
        layout.extend(stage)
    perm = [layout.index(name) for name in FSDP_AXES]
    rank = len(FSDP_AXES)
    gathered = gathered.transpose(perm + [rank, rank + 1])
    return gathered.reshape(-1, shard.shape[1])


def gather_sp(block):
    count = lax.axis_size("sp")
    here = lax.axis_index("sp")
    pieces = [block]
    for shift in range(1, count):
        pairs = [(source, (source + shift) % count) for source in range(count)]
        pieces.append(lax.ppermute(block, "sp", perm=pairs))
    stacked = jnp.stack(pieces)
    order = (here - jnp.arange(count, dtype=jnp.int32)) % count
    return jnp.take(stacked, order, axis=0)


def per_device(
    hidden_rows, queries, key_weight, value_weight, cache_keys, cache_values, span_index, prefix_len
):
    span_rows = hidden_rows.shape[0]
    model_width = hidden_rows.shape[1]
    query_rows = queries.shape[0]
    kv_cols = key_weight.shape[1]
    kv_local = kv_cols // HD
    group_size = HQ // KVH
    slot_total = cache_keys.shape[1]
    sp_index = lax.axis_index("sp")
    block_start = span_index[0] * span_rows
    positions = (block_start + jnp.arange(span_rows, dtype=jnp.int32)).astype(jnp.float32)
    cosine_table, sine_table = yarn_tables(positions, HD)
    first_query = sp_index * query_rows
    query_positions = (
        block_start + first_query + jnp.arange(query_rows, dtype=jnp.int32)
    ).astype(jnp.float32)
    query_cosine, query_sine = yarn_tables(query_positions, HD)
    live_count = prefix_len[0]

    cache_kv = jnp.concatenate([cache_keys[0], cache_values[0]], axis=1)

    whole_kv = gather_weights(jnp.concatenate([key_weight, value_weight], axis=1))
    kv_sum = jnp.dot(hidden_rows, whole_kv[:model_width], preferred_element_type=jnp.float32)
    new_keys = rotate(kv_sum[:, :kv_cols], cosine_table, sine_table, kv_local).astype(jnp.bfloat16)
    new_values = kv_sum[:, kv_cols:].astype(jnp.bfloat16)
    local_kv = jnp.concatenate(
        [cache_kv, jnp.concatenate([new_keys, new_values], axis=1)], axis=0
    )
    every_kv = gather_sp(local_kv)
    cache_all = every_kv[:, :slot_total]
    new_all = every_kv[:, slot_total:]

    rotated_q = rotate(queries.astype(jnp.float32), query_cosine, query_sine, HQ).astype(
        jnp.bfloat16
    )
    query_heads = rotated_q.reshape(query_rows, KVH, group_size, HD)
    scale = HD ** (-0.5)
    old_keys = cache_all[:, :, :HD]
    old_values = cache_all[:, :, HD:]
    fresh_keys = new_all[:, :, :HD]
    fresh_values = new_all[:, :, HD:]
    old_scores = jnp.einsum(
        "thgd,hjd->hgtj", query_heads, old_keys, preferred_element_type=jnp.float32
    ) * scale
    new_scores = jnp.einsum(
        "thgd,hud->hgtu", query_heads, fresh_keys, preferred_element_type=jnp.float32
    ) * scale
    slot_index = jnp.arange(slot_total, dtype=jnp.int32)
    old_visible = (slot_index >= slot_total - live_count)[None, None, None, :]
    key_index = jnp.arange(span_rows, dtype=jnp.int32)
    query_index = first_query + jnp.arange(query_rows, dtype=jnp.int32)
    new_visible = (key_index[None, :] <= query_index[:, None])[None, None, :, :]
    old_scores = jnp.where(old_visible, old_scores, -1e30)
    new_scores = jnp.where(new_visible, new_scores, -1e30)
    row_max = jnp.maximum(jnp.max(old_scores, axis=-1), jnp.max(new_scores, axis=-1))[..., None]
    old_weights = jnp.where(old_visible, jnp.exp(old_scores - row_max), 0.0)
    new_weights = jnp.where(new_visible, jnp.exp(new_scores - row_max), 0.0)
    total = jnp.sum(old_weights, axis=-1) + jnp.sum(new_weights, axis=-1)
    summed = jnp.einsum(
        "hgtj,hjd->hgtd",
        old_weights.astype(jnp.bfloat16),
        old_values,
        preferred_element_type=jnp.float32,
    ) + jnp.einsum(
        "hgtu,hud->hgtd",
        new_weights.astype(jnp.bfloat16),
        fresh_values,
        preferred_element_type=jnp.float32,
    )
    result = (summed / total[..., None]).astype(jnp.bfloat16)
    return result.transpose(2, 0, 1, 3).reshape(query_rows, HQ * HD)


def solution(mesh):
    sizes = tuple(size for _, size in FSDP_PARTS)
    fine = jax.sharding.Mesh(
        mesh.devices.reshape(sizes + (mesh.shape["sp"],)), FSDP_AXES + ("sp",)
    )
    fsdp = FSDP_AXES
    placed = (
        P(fsdp, None),
        P(fsdp + ("sp",), None),
        P(fsdp, "sp"),
        P(fsdp, "sp"),
        P(fsdp, None, "sp"),
        P(fsdp, None, "sp"),
        P(fsdp),
        P(fsdp),
    )
    return jax.shard_map(
        per_device, mesh=fine, in_specs=placed, out_specs=P(fsdp + ("sp",), None), check_vma=False
    )
```

```python
import math

import jax
import jax.numpy as jnp
from jax import lax
from jax.sharding import PartitionSpec as P

HD = 128
HQ = 32
KVH = 4
YARN_SCALE = 16
ORIG_CTX = 8192


rope_base = 500000.0
beta_fast = 32.0
beta_slow = 1.0


def yarn_tables(positions, head_size):
    half_size = head_size // 2
    index_row = jnp.arange(half_size, dtype=jnp.float32)
    inverse = jnp.power(rope_base, -2.0 * index_row / head_size)
    wavelength = 2.0 * math.pi / inverse
    ratio = ORIG_CTX / wavelength
    ramp = jnp.clip((ratio - beta_slow) / (beta_fast - beta_slow), 0.0, 1.0)
    freq = inverse / YARN_SCALE * (1.0 - ramp) + inverse * ramp
    factor = 0.1 * math.log(YARN_SCALE) + 1.0
    angles = positions[:, None] * freq[None, :]
    return (jnp.cos(angles) * factor, jnp.sin(angles) * factor)


def rotate(values, cosine_table, sine_table, head_count):
    row_count = values.shape[0]
    half_size = cosine_table.shape[1]
    split = values.reshape(row_count, head_count, 2, half_size)
    first_half = split[:, :, 0]
    second_half = split[:, :, 1]
    cos_part = cosine_table[:, None, :]
    sin_part = sine_table[:, None, :]
    joined = jnp.stack(
        [
            first_half * cos_part - second_half * sin_part,
            second_half * cos_part + first_half * sin_part,
        ],
        axis=2,
    )
    return joined.reshape(row_count, head_count * 2 * half_size)


def attend_block(state, query_heads, key_block, value_block, visible):
    running_max, running_sum, weighted = state
    block_len = key_block.shape[0]
    kv_heads = query_heads.shape[0]
    key_heads = key_block.reshape(block_len, kv_heads, HD)
    value_heads = value_block.reshape(block_len, kv_heads, HD)
    scores = jnp.einsum(
        "hgqd,khd->hgqk", query_heads, key_heads, preferred_element_type=jnp.float32
    ) * HD ** (-0.5)
    scores = jnp.where(visible, scores, -1e30)
    new_max = jnp.maximum(running_max, jnp.max(scores, axis=-1))
    rescale = jnp.exp(running_max - new_max)
    weights = jnp.where(visible, jnp.exp(scores - new_max[..., None]), 0.0)
    running_sum = running_sum * rescale + jnp.sum(weights, axis=-1)
    product = jnp.einsum(
        "hgqk,khd->hgqd",
        weights.astype(jnp.bfloat16),
        value_heads,
        preferred_element_type=jnp.float32,
    )
    weighted = weighted * rescale[..., None] + product
    return (new_max, running_sum, weighted)


def attend_all(query_heads, old_keys, old_values, new_keys, new_values, live_count):
    kv_heads, group_size, query_rows, head_size = query_heads.shape
    slot_total = old_keys.shape[0]
    span_rows = new_keys.shape[0]
    state = (
        jnp.full((kv_heads, group_size, query_rows), -1e30, jnp.float32),
        jnp.zeros((kv_heads, group_size, query_rows), jnp.float32),
        jnp.zeros((kv_heads, group_size, query_rows, head_size), jnp.float32),
    )
    cache_block = min(256, slot_total)

    def cache_step(block_number, carried):
        start = block_number * cache_block
        slot_index = start + jnp.arange(cache_block, dtype=jnp.int32)
        visible = (slot_index >= slot_total - live_count)[None, None, None, :]
        return attend_block(carried, query_heads, old_keys, old_values, visible)

    state = lax.fori_loop(0, slot_total // cache_block, cache_step, state)
    new_block = min(256, span_rows)
    query_index = jnp.arange(query_rows, dtype=jnp.int32)

    def new_step(block_number, carried):
        start = block_number * new_block
        key_block = lax.dynamic_slice_in_dim(new_keys, start, new_block, 0)
        value_block = lax.dynamic_slice_in_dim(new_values, start, new_block, 0)
        key_index = start + jnp.arange(new_block, dtype=jnp.int32)
        visible = (key_index[None, :] <= query_index[:, None])[None, None, :, :]
        return attend_block(carried, query_heads, key_block, value_block, visible)

    state = lax.fori_loop(0, span_rows // new_block, new_step, state)
    running_max, running_sum, weighted = state
    result = (weighted / running_sum[..., None]).astype(jnp.bfloat16)
    return result.transpose(2, 0, 1, 3).reshape(query_rows, kv_heads * group_size * head_size)


FSDP_PARTS = (("ylo", 2), ("x", 4), ("z", 12), ("core", 2))
FSDP_AXES = tuple(name for name, _ in FSDP_PARTS)
GATHER_STAGES = (("ylo",), ("x",), ("z",), ("core",))


def gather_weights(shard):
    gathered = shard
    for stage in GATHER_STAGES:
        gathered = lax.all_gather(gathered, stage, axis=0, tiled=False)
        if len(stage) > 1:
            sizes = tuple(dict(FSDP_PARTS)[name] for name in stage)
            gathered = gathered.reshape(sizes + gathered.shape[1:])
    layout = []
    for stage in reversed(GATHER_STAGES):
        layout.extend(stage)
    perm = [layout.index(name) for name in FSDP_AXES]
    rank = len(FSDP_AXES)
    gathered = gathered.transpose(perm + [rank, rank + 1])
    return gathered.reshape(-1, shard.shape[1])


def gather_sp(block):
    count = lax.axis_size("sp")
    here = lax.axis_index("sp")
    pieces = [block]
    for shift in range(1, count):
        pairs = [(source, (source + shift) % count) for source in range(count)]
        pieces.append(lax.ppermute(block, "sp", perm=pairs))
    stacked = jnp.stack(pieces)
    order = (here - jnp.arange(count, dtype=jnp.int32)) % count
    return jnp.take(stacked, order, axis=0)


def gather_sp_relay(block):
    count = lax.axis_size("sp")
    if count != 4:
        return gather_sp(block)
    here = lax.axis_index("sp")
    forward = [(source, (source + 1) % count) for source in range(count)]
    backward = [(source, (source - 1) % count) for source in range(count)]
    from_left = lax.ppermute(block, "sp", perm=forward)
    from_right = lax.ppermute(block, "sp", perm=backward)
    half = block.shape[1] // 2
    far_first = lax.ppermute(from_left[:, :half], "sp", perm=forward)
    far_second = lax.ppermute(from_right[:, half:], "sp", perm=backward)
    far = jnp.concatenate([far_first, far_second], axis=1)
    stacked = jnp.stack([block, from_left, far, from_right])
    order = (here - jnp.arange(count, dtype=jnp.int32)) % count
    return jnp.take(stacked, order, axis=0)


def per_device(
    hidden_rows, queries, key_weight, value_weight, cache_keys, cache_values, span_index, prefix_len
):
    span_rows = hidden_rows.shape[0]
    model_width = hidden_rows.shape[1]
    query_rows = queries.shape[0]
    kv_cols = key_weight.shape[1]
    kv_local = kv_cols // HD
    group_size = HQ // KVH
    slot_total = cache_keys.shape[1]
    sp_index = lax.axis_index("sp")
    block_start = span_index[0] * span_rows
    positions = (block_start + jnp.arange(span_rows, dtype=jnp.int32)).astype(jnp.float32)
    cosine_table, sine_table = yarn_tables(positions, HD)
    first_query = sp_index * query_rows
    query_positions = (
        block_start + first_query + jnp.arange(query_rows, dtype=jnp.int32)
    ).astype(jnp.float32)
    query_cosine, query_sine = yarn_tables(query_positions, HD)
    live_count = prefix_len[0]

    cache_kv = jnp.concatenate([cache_keys[0], cache_values[0]], axis=1)
    cache_all = gather_sp(cache_kv)

    whole_kv = gather_weights(jnp.concatenate([key_weight, value_weight], axis=1))
    kv_sum = jnp.dot(hidden_rows, whole_kv[:model_width], preferred_element_type=jnp.float32)
    new_keys = rotate(kv_sum[:, :kv_cols], cosine_table, sine_table, kv_local).astype(jnp.bfloat16)
    new_values = kv_sum[:, kv_cols:].astype(jnp.bfloat16)
    new_all = gather_sp_relay(jnp.concatenate([new_keys, new_values], axis=1))

    rotated_q = rotate(queries.astype(jnp.float32), query_cosine, query_sine, HQ).astype(
        jnp.bfloat16
    )
    query_heads = rotated_q.reshape(query_rows, KVH, group_size, HD)
    scale = HD ** (-0.5)
    old_keys = cache_all[:, :, :HD]
    old_values = cache_all[:, :, HD:]
    fresh_keys = new_all[:, :, :HD]
    fresh_values = new_all[:, :, HD:]
    old_scores = jnp.einsum(
        "thgd,hjd->hgtj", query_heads, old_keys, preferred_element_type=jnp.float32
    ) * scale
    new_scores = jnp.einsum(
        "thgd,hud->hgtu", query_heads, fresh_keys, preferred_element_type=jnp.float32
    ) * scale
    slot_index = jnp.arange(slot_total, dtype=jnp.int32)
    old_visible = (slot_index >= slot_total - live_count)[None, None, None, :]
    key_index = jnp.arange(span_rows, dtype=jnp.int32)
    query_index = first_query + jnp.arange(query_rows, dtype=jnp.int32)
    new_visible = (key_index[None, :] <= query_index[:, None])[None, None, :, :]
    old_scores = jnp.where(old_visible, old_scores, -1e30)
    new_scores = jnp.where(new_visible, new_scores, -1e30)
    row_max = jnp.maximum(jnp.max(old_scores, axis=-1), jnp.max(new_scores, axis=-1))[..., None]
    old_weights = jnp.where(old_visible, jnp.exp(old_scores - row_max), 0.0)
    new_weights = jnp.where(new_visible, jnp.exp(new_scores - row_max), 0.0)
    total = jnp.sum(old_weights, axis=-1) + jnp.sum(new_weights, axis=-1)
    summed = jnp.einsum(
        "hgtj,hjd->hgtd",
        old_weights.astype(jnp.bfloat16),
        old_values,
        preferred_element_type=jnp.float32,
    ) + jnp.einsum(
        "hgtu,hud->hgtd",
        new_weights.astype(jnp.bfloat16),
        fresh_values,
        preferred_element_type=jnp.float32,
    )
    result = (summed / total[..., None]).astype(jnp.bfloat16)
    return result.transpose(2, 0, 1, 3).reshape(query_rows, HQ * HD)


def solution(mesh):
    sizes = tuple(size for _, size in FSDP_PARTS)
    fine = jax.sharding.Mesh(
        mesh.devices.reshape(sizes + (mesh.shape["sp"],)), FSDP_AXES + ("sp",)
    )
    fsdp = FSDP_AXES
    placed = (
        P(fsdp, None),
        P(fsdp + ("sp",), None),
        P(fsdp, "sp"),
        P(fsdp, "sp"),
        P(fsdp, None, "sp"),
        P(fsdp, None, "sp"),
        P(fsdp),
        P(fsdp),
    )
    return jax.shard_map(
        per_device, mesh=fine, in_specs=placed, out_specs=P(fsdp + ("sp",), None), check_vma=False
    )
```

```python
import math

import jax
import jax.numpy as jnp
from jax import lax
from jax.sharding import PartitionSpec as P

HD = 128
HQ = 32
KVH = 4
YARN_SCALE = 16
ORIG_CTX = 8192


rope_base = 500000.0
beta_fast = 32.0
beta_slow = 1.0


def yarn_tables(positions, head_size):
    half_size = head_size // 2
    index_row = jnp.arange(half_size, dtype=jnp.float32)
    inverse = jnp.power(rope_base, -2.0 * index_row / head_size)
    wavelength = 2.0 * math.pi / inverse
    ratio = ORIG_CTX / wavelength
    ramp = jnp.clip((ratio - beta_slow) / (beta_fast - beta_slow), 0.0, 1.0)
    freq = inverse / YARN_SCALE * (1.0 - ramp) + inverse * ramp
    factor = 0.1 * math.log(YARN_SCALE) + 1.0
    angles = positions[:, None] * freq[None, :]
    return (jnp.cos(angles) * factor, jnp.sin(angles) * factor)


def rotate(values, cosine_table, sine_table, head_count):
    row_count = values.shape[0]
    half_size = cosine_table.shape[1]
    split = values.reshape(row_count, head_count, 2, half_size)
    first_half = split[:, :, 0]
    second_half = split[:, :, 1]
    cos_part = cosine_table[:, None, :]
    sin_part = sine_table[:, None, :]
    joined = jnp.stack(
        [
            first_half * cos_part - second_half * sin_part,
            second_half * cos_part + first_half * sin_part,
        ],
        axis=2,
    )
    return joined.reshape(row_count, head_count * 2 * half_size)


def attend_block(state, query_heads, key_block, value_block, visible):
    running_max, running_sum, weighted = state
    block_len = key_block.shape[0]
    kv_heads = query_heads.shape[0]
    key_heads = key_block.reshape(block_len, kv_heads, HD)
    value_heads = value_block.reshape(block_len, kv_heads, HD)
    scores = jnp.einsum(
        "hgqd,khd->hgqk", query_heads, key_heads, preferred_element_type=jnp.float32
    ) * HD ** (-0.5)
    scores = jnp.where(visible, scores, -1e30)
    new_max = jnp.maximum(running_max, jnp.max(scores, axis=-1))
    rescale = jnp.exp(running_max - new_max)
    weights = jnp.where(visible, jnp.exp(scores - new_max[..., None]), 0.0)
    running_sum = running_sum * rescale + jnp.sum(weights, axis=-1)
    product = jnp.einsum(
        "hgqk,khd->hgqd",
        weights.astype(jnp.bfloat16),
        value_heads,
        preferred_element_type=jnp.float32,
    )
    weighted = weighted * rescale[..., None] + product
    return (new_max, running_sum, weighted)


def attend_all(query_heads, old_keys, old_values, new_keys, new_values, live_count):
    kv_heads, group_size, query_rows, head_size = query_heads.shape
    slot_total = old_keys.shape[0]
    span_rows = new_keys.shape[0]
    state = (
        jnp.full((kv_heads, group_size, query_rows), -1e30, jnp.float32),
        jnp.zeros((kv_heads, group_size, query_rows), jnp.float32),
        jnp.zeros((kv_heads, group_size, query_rows, head_size), jnp.float32),
    )
    cache_block = min(256, slot_total)

    def cache_step(block_number, carried):
        start = block_number * cache_block
        slot_index = start + jnp.arange(cache_block, dtype=jnp.int32)
        visible = (slot_index >= slot_total - live_count)[None, None, None, :]
        return attend_block(carried, query_heads, old_keys, old_values, visible)

    state = lax.fori_loop(0, slot_total // cache_block, cache_step, state)
    new_block = min(256, span_rows)
    query_index = jnp.arange(query_rows, dtype=jnp.int32)

    def new_step(block_number, carried):
        start = block_number * new_block
        key_block = lax.dynamic_slice_in_dim(new_keys, start, new_block, 0)
        value_block = lax.dynamic_slice_in_dim(new_values, start, new_block, 0)
        key_index = start + jnp.arange(new_block, dtype=jnp.int32)
        visible = (key_index[None, :] <= query_index[:, None])[None, None, :, :]
        return attend_block(carried, query_heads, key_block, value_block, visible)

    state = lax.fori_loop(0, span_rows // new_block, new_step, state)
    running_max, running_sum, weighted = state
    result = (weighted / running_sum[..., None]).astype(jnp.bfloat16)
    return result.transpose(2, 0, 1, 3).reshape(query_rows, kv_heads * group_size * head_size)


FSDP_PARTS = (("ylo", 2), ("x", 4), ("z", 12), ("core", 2))
FSDP_AXES = tuple(name for name, _ in FSDP_PARTS)
GATHER_STAGES = (("ylo",), ("x",), ("z",), ("core",))


def gather_weights(shard):
    gathered = shard
    for stage in GATHER_STAGES[:-1]:
        gathered = lax.all_gather(gathered, stage, axis=0, tiled=False)
    early = [name for stage in reversed(GATHER_STAGES[:-1]) for name in stage]
    wanted = [name for name in FSDP_AXES if name in early]
    rank = len(early)
    gathered = gathered.transpose([early.index(name) for name in wanted] + [rank, rank + 1])
    (last,) = GATHER_STAGES[-1]
    gathered = lax.all_gather(gathered, last, axis=FSDP_AXES.index(last), tiled=False)
    return gathered.reshape(-1, shard.shape[1])


def gather_sp(block):
    count = lax.axis_size("sp")
    here = lax.axis_index("sp")
    pieces = [block]
    for shift in range(1, count):
        pairs = [(source, (source + shift) % count) for source in range(count)]
        pieces.append(lax.ppermute(block, "sp", perm=pairs))
    stacked = jnp.stack(pieces)
    order = (here - jnp.arange(count, dtype=jnp.int32)) % count
    return jnp.take(stacked, order, axis=0)


def per_device(
    hidden_rows, queries, key_weight, value_weight, cache_keys, cache_values, span_index, prefix_len
):
    span_rows = hidden_rows.shape[0]
    model_width = hidden_rows.shape[1]
    query_rows = queries.shape[0]
    kv_cols = key_weight.shape[1]
    kv_local = kv_cols // HD
    group_size = HQ // KVH
    slot_total = cache_keys.shape[1]
    sp_index = lax.axis_index("sp")
    block_start = span_index[0] * span_rows
    positions = (block_start + jnp.arange(span_rows, dtype=jnp.int32)).astype(jnp.float32)
    cosine_table, sine_table = yarn_tables(positions, HD)
    first_query = sp_index * query_rows
    query_positions = (
        block_start + first_query + jnp.arange(query_rows, dtype=jnp.int32)
    ).astype(jnp.float32)
    query_cosine, query_sine = yarn_tables(query_positions, HD)
    live_count = prefix_len[0]

    cache_kv = jnp.concatenate([cache_keys[0], cache_values[0]], axis=1)
    cache_all = gather_sp(cache_kv)

    whole_kv = gather_weights(jnp.concatenate([key_weight, value_weight], axis=1))
    kv_sum = jnp.dot(hidden_rows, whole_kv[:model_width], preferred_element_type=jnp.float32)
    new_keys = rotate(kv_sum[:, :kv_cols], cosine_table, sine_table, kv_local).astype(jnp.bfloat16)
    new_values = kv_sum[:, kv_cols:].astype(jnp.bfloat16)
    new_all = gather_sp(jnp.concatenate([new_keys, new_values], axis=1))

    rotated_q = rotate(queries.astype(jnp.float32), query_cosine, query_sine, HQ).astype(
        jnp.bfloat16
    )
    query_heads = rotated_q.reshape(query_rows, KVH, group_size, HD)
    scale = HD ** (-0.5)
    old_keys = cache_all[:, :, :HD]
    old_values = cache_all[:, :, HD:]
    fresh_keys = new_all[:, :, :HD]
    fresh_values = new_all[:, :, HD:]
    old_scores = jnp.einsum(
        "thgd,hjd->hgtj", query_heads, old_keys, preferred_element_type=jnp.float32
    ) * scale
    new_scores = jnp.einsum(
        "thgd,hud->hgtu", query_heads, fresh_keys, preferred_element_type=jnp.float32
    ) * scale
    slot_index = jnp.arange(slot_total, dtype=jnp.int32)
    old_visible = (slot_index >= slot_total - live_count)[None, None, None, :]
    key_index = jnp.arange(span_rows, dtype=jnp.int32)
    query_index = first_query + jnp.arange(query_rows, dtype=jnp.int32)
    new_visible = (key_index[None, :] <= query_index[:, None])[None, None, :, :]
    old_scores = jnp.where(old_visible, old_scores, -1e30)
    new_scores = jnp.where(new_visible, new_scores, -1e30)
    row_max = jnp.maximum(jnp.max(old_scores, axis=-1), jnp.max(new_scores, axis=-1))[..., None]
    old_weights = jnp.where(old_visible, jnp.exp(old_scores - row_max), 0.0)
    new_weights = jnp.where(new_visible, jnp.exp(new_scores - row_max), 0.0)
    total = jnp.sum(old_weights, axis=-1) + jnp.sum(new_weights, axis=-1)
    summed = jnp.einsum(
        "hgtj,hjd->hgtd",
        old_weights.astype(jnp.bfloat16),
        old_values,
        preferred_element_type=jnp.float32,
    ) + jnp.einsum(
        "hgtu,hud->hgtd",
        new_weights.astype(jnp.bfloat16),
        fresh_values,
        preferred_element_type=jnp.float32,
    )
    result = (summed / total[..., None]).astype(jnp.bfloat16)
    return result.transpose(2, 0, 1, 3).reshape(query_rows, HQ * HD)


def solution(mesh):
    sizes = tuple(size for _, size in FSDP_PARTS)
    fine = jax.sharding.Mesh(
        mesh.devices.reshape(sizes + (mesh.shape["sp"],)), FSDP_AXES + ("sp",)
    )
    fsdp = FSDP_AXES
    placed = (
        P(fsdp, None),
        P(fsdp + ("sp",), None),
        P(fsdp, "sp"),
        P(fsdp, "sp"),
        P(fsdp, None, "sp"),
        P(fsdp, None, "sp"),
        P(fsdp),
        P(fsdp),
    )
    return jax.shard_map(
        per_device, mesh=fine, in_specs=placed, out_specs=P(fsdp + ("sp",), None), check_vma=False
    )
```

```python
import math

import jax
import jax.numpy as jnp
from jax import lax
from jax.sharding import PartitionSpec as P

HD = 128
HQ = 32
KVH = 4
YARN_SCALE = 16
ORIG_CTX = 8192


rope_base = 500000.0
beta_fast = 32.0
beta_slow = 1.0


def yarn_tables(positions, head_size):
    half_size = head_size // 2
    index_row = jnp.arange(half_size, dtype=jnp.float32)
    inverse = jnp.power(rope_base, -2.0 * index_row / head_size)
    wavelength = 2.0 * math.pi / inverse
    ratio = ORIG_CTX / wavelength
    ramp = jnp.clip((ratio - beta_slow) / (beta_fast - beta_slow), 0.0, 1.0)
    freq = inverse / YARN_SCALE * (1.0 - ramp) + inverse * ramp
    factor = 0.1 * math.log(YARN_SCALE) + 1.0
    angles = positions[:, None] * freq[None, :]
    return (jnp.cos(angles) * factor, jnp.sin(angles) * factor)


def rotate(values, cosine_table, sine_table, head_count):
    row_count = values.shape[0]
    half_size = cosine_table.shape[1]
    split = values.reshape(row_count, head_count, 2, half_size)
    first_half = split[:, :, 0]
    second_half = split[:, :, 1]
    cos_part = cosine_table[:, None, :]
    sin_part = sine_table[:, None, :]
    joined = jnp.stack(
        [
            first_half * cos_part - second_half * sin_part,
            second_half * cos_part + first_half * sin_part,
        ],
        axis=2,
    )
    return joined.reshape(row_count, head_count * 2 * half_size)


def attend_block(state, query_heads, key_block, value_block, visible):
    running_max, running_sum, weighted = state
    block_len = key_block.shape[0]
    kv_heads = query_heads.shape[0]
    key_heads = key_block.reshape(block_len, kv_heads, HD)
    value_heads = value_block.reshape(block_len, kv_heads, HD)
    scores = jnp.einsum(
        "hgqd,khd->hgqk", query_heads, key_heads, preferred_element_type=jnp.float32
    ) * HD ** (-0.5)
    scores = jnp.where(visible, scores, -1e30)
    new_max = jnp.maximum(running_max, jnp.max(scores, axis=-1))
    rescale = jnp.exp(running_max - new_max)
    weights = jnp.where(visible, jnp.exp(scores - new_max[..., None]), 0.0)
    running_sum = running_sum * rescale + jnp.sum(weights, axis=-1)
    product = jnp.einsum(
        "hgqk,khd->hgqd",
        weights.astype(jnp.bfloat16),
        value_heads,
        preferred_element_type=jnp.float32,
    )
    weighted = weighted * rescale[..., None] + product
    return (new_max, running_sum, weighted)


def attend_all(query_heads, old_keys, old_values, new_keys, new_values, live_count):
    kv_heads, group_size, query_rows, head_size = query_heads.shape
    slot_total = old_keys.shape[0]
    span_rows = new_keys.shape[0]
    state = (
        jnp.full((kv_heads, group_size, query_rows), -1e30, jnp.float32),
        jnp.zeros((kv_heads, group_size, query_rows), jnp.float32),
        jnp.zeros((kv_heads, group_size, query_rows, head_size), jnp.float32),
    )
    cache_block = min(256, slot_total)

    def cache_step(block_number, carried):
        start = block_number * cache_block
        slot_index = start + jnp.arange(cache_block, dtype=jnp.int32)
        visible = (slot_index >= slot_total - live_count)[None, None, None, :]
        return attend_block(carried, query_heads, old_keys, old_values, visible)

    state = lax.fori_loop(0, slot_total // cache_block, cache_step, state)
    new_block = min(256, span_rows)
    query_index = jnp.arange(query_rows, dtype=jnp.int32)

    def new_step(block_number, carried):
        start = block_number * new_block
        key_block = lax.dynamic_slice_in_dim(new_keys, start, new_block, 0)
        value_block = lax.dynamic_slice_in_dim(new_values, start, new_block, 0)
        key_index = start + jnp.arange(new_block, dtype=jnp.int32)
        visible = (key_index[None, :] <= query_index[:, None])[None, None, :, :]
        return attend_block(carried, query_heads, key_block, value_block, visible)

    state = lax.fori_loop(0, span_rows // new_block, new_step, state)
    running_max, running_sum, weighted = state
    result = (weighted / running_sum[..., None]).astype(jnp.bfloat16)
    return result.transpose(2, 0, 1, 3).reshape(query_rows, kv_heads * group_size * head_size)


FSDP_PARTS = (("ylo", 2), ("x", 4), ("z", 12), ("core", 2))
FSDP_AXES = tuple(name for name, _ in FSDP_PARTS)
GATHER_STAGES = (("ylo",), ("x",), ("z",), ("core",))


def gather_weights(shard):
    gathered = shard
    for stage in GATHER_STAGES[:-1]:
        gathered = lax.all_gather(gathered, stage, axis=0, tiled=False)
    early = [name for stage in reversed(GATHER_STAGES[:-1]) for name in stage]
    wanted = [name for name in FSDP_AXES if name in early]
    rank = len(early)
    gathered = gathered.transpose([early.index(name) for name in wanted] + [rank, rank + 1])
    (last,) = GATHER_STAGES[-1]
    gathered = lax.all_gather(gathered, last, axis=FSDP_AXES.index(last), tiled=False)
    return gathered.reshape(-1, shard.shape[1])


def gather_sp(block):
    count = lax.axis_size("sp")
    here = lax.axis_index("sp")
    pieces = [block]
    for shift in range(1, count):
        pairs = [(source, (source + shift) % count) for source in range(count)]
        pieces.append(lax.ppermute(block, "sp", perm=pairs))
    stacked = jnp.stack(pieces)
    order = (here - jnp.arange(count, dtype=jnp.int32)) % count
    return jnp.take(stacked, order, axis=0)


def per_device(
    hidden_rows, queries, key_weight, value_weight, cache_keys, cache_values, span_index, prefix_len
):
    span_rows = hidden_rows.shape[0]
    model_width = hidden_rows.shape[1]
    query_rows = queries.shape[0]
    kv_cols = key_weight.shape[1]
    kv_local = kv_cols // HD
    group_size = HQ // KVH
    slot_total = cache_keys.shape[1]
    sp_index = lax.axis_index("sp")
    block_start = span_index[0] * span_rows
    positions = (block_start + jnp.arange(span_rows, dtype=jnp.int32)).astype(jnp.float32)
    cosine_table, sine_table = yarn_tables(positions, HD)
    first_query = sp_index * query_rows
    query_positions = (
        block_start + first_query + jnp.arange(query_rows, dtype=jnp.int32)
    ).astype(jnp.float32)
    query_cosine, query_sine = yarn_tables(query_positions, HD)
    live_count = prefix_len[0]

    cache_kv = jnp.concatenate([cache_keys[0], cache_values[0]], axis=1)
    cache_all = gather_sp(cache_kv)

    whole_kv = gather_weights(jnp.concatenate([key_weight, value_weight], axis=1))
    kv_sum = jnp.dot(hidden_rows, whole_kv[:model_width], preferred_element_type=jnp.float32)
    new_keys = rotate(kv_sum[:, :kv_cols], cosine_table, sine_table, kv_local).astype(jnp.bfloat16)
    new_values = kv_sum[:, kv_cols:].astype(jnp.bfloat16)
    new_kv = jnp.concatenate([new_keys, new_values], axis=1)
    repeated = jnp.broadcast_to(new_kv[None], (lax.axis_size("sp"),) + new_kv.shape)
    new_all = lax.all_to_all(repeated, "sp", split_axis=0, concat_axis=0, tiled=True)

    rotated_q = rotate(queries.astype(jnp.float32), query_cosine, query_sine, HQ).astype(
        jnp.bfloat16
    )
    query_heads = rotated_q.reshape(query_rows, KVH, group_size, HD)
    scale = HD ** (-0.5)
    old_keys = cache_all[:, :, :HD]
    old_values = cache_all[:, :, HD:]
    fresh_keys = new_all[:, :, :HD]
    fresh_values = new_all[:, :, HD:]
    old_scores = jnp.einsum(
        "thgd,hjd->hgtj", query_heads, old_keys, preferred_element_type=jnp.float32
    ) * scale
    new_scores = jnp.einsum(
        "thgd,hud->hgtu", query_heads, fresh_keys, preferred_element_type=jnp.float32
    ) * scale
    slot_index = jnp.arange(slot_total, dtype=jnp.int32)
    old_visible = (slot_index >= slot_total - live_count)[None, None, None, :]
    key_index = jnp.arange(span_rows, dtype=jnp.int32)
    query_index = first_query + jnp.arange(query_rows, dtype=jnp.int32)
    new_visible = (key_index[None, :] <= query_index[:, None])[None, None, :, :]
    old_scores = jnp.where(old_visible, old_scores, -1e30)
    new_scores = jnp.where(new_visible, new_scores, -1e30)
    row_max = jnp.maximum(jnp.max(old_scores, axis=-1), jnp.max(new_scores, axis=-1))[..., None]
    old_weights = jnp.where(old_visible, jnp.exp(old_scores - row_max), 0.0)
    new_weights = jnp.where(new_visible, jnp.exp(new_scores - row_max), 0.0)
    total = jnp.sum(old_weights, axis=-1) + jnp.sum(new_weights, axis=-1)
    summed = jnp.einsum(
        "hgtj,hjd->hgtd",
        old_weights.astype(jnp.bfloat16),
        old_values,
        preferred_element_type=jnp.float32,
    ) + jnp.einsum(
        "hgtu,hud->hgtd",
        new_weights.astype(jnp.bfloat16),
        fresh_values,
        preferred_element_type=jnp.float32,
    )
    result = (summed / total[..., None]).astype(jnp.bfloat16)
    return result.transpose(2, 0, 1, 3).reshape(query_rows, HQ * HD)


def solution(mesh):
    sizes = tuple(size for _, size in FSDP_PARTS)
    fine = jax.sharding.Mesh(
        mesh.devices.reshape(sizes + (mesh.shape["sp"],)), FSDP_AXES + ("sp",)
    )
    fsdp = FSDP_AXES
    placed = (
        P(fsdp, None),
        P(fsdp + ("sp",), None),
        P(fsdp, "sp"),
        P(fsdp, "sp"),
        P(fsdp, None, "sp"),
        P(fsdp, None, "sp"),
        P(fsdp),
        P(fsdp),
    )
    return jax.shard_map(
        per_device, mesh=fine, in_specs=placed, out_specs=P(fsdp + ("sp",), None), check_vma=False
    )
```

```python
import math

import jax
import jax.numpy as jnp
from jax import lax
from jax.sharding import PartitionSpec as P

HD = 128
HQ = 32
KVH = 4
YARN_SCALE = 16
ORIG_CTX = 8192


rope_base = 500000.0
beta_fast = 32.0
beta_slow = 1.0


def yarn_tables(positions, head_size):
    half_size = head_size // 2
    index_row = jnp.arange(half_size, dtype=jnp.float32)
    inverse = jnp.power(rope_base, -2.0 * index_row / head_size)
    wavelength = 2.0 * math.pi / inverse
    ratio = ORIG_CTX / wavelength
    ramp = jnp.clip((ratio - beta_slow) / (beta_fast - beta_slow), 0.0, 1.0)
    freq = inverse / YARN_SCALE * (1.0 - ramp) + inverse * ramp
    factor = 0.1 * math.log(YARN_SCALE) + 1.0
    angles = positions[:, None] * freq[None, :]
    return (jnp.cos(angles) * factor, jnp.sin(angles) * factor)


def rotate(values, cosine_table, sine_table, head_count):
    row_count = values.shape[0]
    half_size = cosine_table.shape[1]
    split = values.reshape(row_count, head_count, 2, half_size)
    first_half = split[:, :, 0]
    second_half = split[:, :, 1]
    cos_part = cosine_table[:, None, :]
    sin_part = sine_table[:, None, :]
    joined = jnp.stack(
        [
            first_half * cos_part - second_half * sin_part,
            second_half * cos_part + first_half * sin_part,
        ],
        axis=2,
    )
    return joined.reshape(row_count, head_count * 2 * half_size)


def attend_block(state, query_heads, key_block, value_block, visible):
    running_max, running_sum, weighted = state
    block_len = key_block.shape[0]
    kv_heads = query_heads.shape[0]
    key_heads = key_block.reshape(block_len, kv_heads, HD)
    value_heads = value_block.reshape(block_len, kv_heads, HD)
    scores = jnp.einsum(
        "hgqd,khd->hgqk", query_heads, key_heads, preferred_element_type=jnp.float32
    ) * HD ** (-0.5)
    scores = jnp.where(visible, scores, -1e30)
    new_max = jnp.maximum(running_max, jnp.max(scores, axis=-1))
    rescale = jnp.exp(running_max - new_max)
    weights = jnp.where(visible, jnp.exp(scores - new_max[..., None]), 0.0)
    running_sum = running_sum * rescale + jnp.sum(weights, axis=-1)
    product = jnp.einsum(
        "hgqk,khd->hgqd",
        weights.astype(jnp.bfloat16),
        value_heads,
        preferred_element_type=jnp.float32,
    )
    weighted = weighted * rescale[..., None] + product
    return (new_max, running_sum, weighted)


def attend_all(query_heads, old_keys, old_values, new_keys, new_values, live_count):
    kv_heads, group_size, query_rows, head_size = query_heads.shape
    slot_total = old_keys.shape[0]
    span_rows = new_keys.shape[0]
    state = (
        jnp.full((kv_heads, group_size, query_rows), -1e30, jnp.float32),
        jnp.zeros((kv_heads, group_size, query_rows), jnp.float32),
        jnp.zeros((kv_heads, group_size, query_rows, head_size), jnp.float32),
    )
    cache_block = min(256, slot_total)

    def cache_step(block_number, carried):
        start = block_number * cache_block
        slot_index = start + jnp.arange(cache_block, dtype=jnp.int32)
        visible = (slot_index >= slot_total - live_count)[None, None, None, :]
        return attend_block(carried, query_heads, old_keys, old_values, visible)

    state = lax.fori_loop(0, slot_total // cache_block, cache_step, state)
    new_block = min(256, span_rows)
    query_index = jnp.arange(query_rows, dtype=jnp.int32)

    def new_step(block_number, carried):
        start = block_number * new_block
        key_block = lax.dynamic_slice_in_dim(new_keys, start, new_block, 0)
        value_block = lax.dynamic_slice_in_dim(new_values, start, new_block, 0)
        key_index = start + jnp.arange(new_block, dtype=jnp.int32)
        visible = (key_index[None, :] <= query_index[:, None])[None, None, :, :]
        return attend_block(carried, query_heads, key_block, value_block, visible)

    state = lax.fori_loop(0, span_rows // new_block, new_step, state)
    running_max, running_sum, weighted = state
    result = (weighted / running_sum[..., None]).astype(jnp.bfloat16)
    return result.transpose(2, 0, 1, 3).reshape(query_rows, kv_heads * group_size * head_size)


FSDP_PARTS = (("ylo", 2), ("x", 4), ("z", 12), ("core", 2))
FSDP_AXES = tuple(name for name, _ in FSDP_PARTS)
GATHER_STAGES = (("ylo",), ("x",), ("z",), ("core",))


def gather_weights(shard):
    gathered = shard
    for stage in GATHER_STAGES[:-1]:
        gathered = lax.all_gather(gathered, stage, axis=0, tiled=False)
    early = [name for stage in reversed(GATHER_STAGES[:-1]) for name in stage]
    wanted = [name for name in FSDP_AXES if name in early]
    rank = len(early)
    gathered = gathered.transpose([early.index(name) for name in wanted] + [rank, rank + 1])
    (last,) = GATHER_STAGES[-1]
    gathered = lax.all_gather(gathered, last, axis=FSDP_AXES.index(last), tiled=False)
    return gathered.reshape(-1, shard.shape[1])


def gather_sp(block):
    count = lax.axis_size("sp")
    here = lax.axis_index("sp")
    pieces = [block]
    for shift in range(1, count):
        pairs = [(source, (source + shift) % count) for source in range(count)]
        pieces.append(lax.ppermute(block, "sp", perm=pairs))
    stacked = jnp.stack(pieces)
    order = (here - jnp.arange(count, dtype=jnp.int32)) % count
    return jnp.take(stacked, order, axis=0)


def exchange_causal(block, query_rows):
    count = lax.axis_size("sp")
    here = lax.axis_index("sp")
    split = block.shape[0] // 2
    head = block[:split]
    repeated = jnp.broadcast_to(head[None], (count,) + head.shape)
    head_all = lax.all_to_all(repeated, "sp", split_axis=0, concat_axis=0, tiled=True)
    tail = block[split:]
    readers = [j for j in range(count) if query_rows * (j + 1) > split]
    pieces = [tail]
    for shift in range(1, count):
        pairs = [((j - shift) % count, j) for j in readers]
        pieces.append(lax.ppermute(tail, "sp", perm=pairs))
    stacked = jnp.stack(pieces)
    order = (here - jnp.arange(count, dtype=jnp.int32)) % count
    tail_all = jnp.take(stacked, order, axis=0)
    return jnp.concatenate([head_all, tail_all], axis=1)


def per_device(
    hidden_rows, queries, key_weight, value_weight, cache_keys, cache_values, span_index, prefix_len
):
    span_rows = hidden_rows.shape[0]
    model_width = hidden_rows.shape[1]
    query_rows = queries.shape[0]
    kv_cols = key_weight.shape[1]
    kv_local = kv_cols // HD
    group_size = HQ // KVH
    slot_total = cache_keys.shape[1]
    sp_index = lax.axis_index("sp")
    block_start = span_index[0] * span_rows
    positions = (block_start + jnp.arange(span_rows, dtype=jnp.int32)).astype(jnp.float32)
    cosine_table, sine_table = yarn_tables(positions, HD)
    first_query = sp_index * query_rows
    query_positions = (
        block_start + first_query + jnp.arange(query_rows, dtype=jnp.int32)
    ).astype(jnp.float32)
    query_cosine, query_sine = yarn_tables(query_positions, HD)
    live_count = prefix_len[0]

    cache_kv = jnp.concatenate([cache_keys[0], cache_values[0]], axis=1)
    cache_all = gather_sp(cache_kv)

    whole_kv = gather_weights(jnp.concatenate([key_weight, value_weight], axis=1))
    kv_sum = jnp.dot(hidden_rows, whole_kv[:model_width], preferred_element_type=jnp.float32)
    new_keys = rotate(kv_sum[:, :kv_cols], cosine_table, sine_table, kv_local).astype(jnp.bfloat16)
    new_values = kv_sum[:, kv_cols:].astype(jnp.bfloat16)
    new_kv = jnp.concatenate([new_keys, new_values], axis=1)
    new_all = exchange_causal(new_kv, query_rows)

    rotated_q = rotate(queries.astype(jnp.float32), query_cosine, query_sine, HQ).astype(
        jnp.bfloat16
    )
    query_heads = rotated_q.reshape(query_rows, KVH, group_size, HD)
    scale = HD ** (-0.5)
    old_keys = cache_all[:, :, :HD]
    old_values = cache_all[:, :, HD:]
    fresh_keys = new_all[:, :, :HD]
    fresh_values = new_all[:, :, HD:]
    old_scores = jnp.einsum(
        "thgd,hjd->hgtj", query_heads, old_keys, preferred_element_type=jnp.float32
    ) * scale
    new_scores = jnp.einsum(
        "thgd,hud->hgtu", query_heads, fresh_keys, preferred_element_type=jnp.float32
    ) * scale
    slot_index = jnp.arange(slot_total, dtype=jnp.int32)
    old_visible = (slot_index >= slot_total - live_count)[None, None, None, :]
    key_index = jnp.arange(span_rows, dtype=jnp.int32)
    query_index = first_query + jnp.arange(query_rows, dtype=jnp.int32)
    new_visible = (key_index[None, :] <= query_index[:, None])[None, None, :, :]
    old_scores = jnp.where(old_visible, old_scores, -1e30)
    new_scores = jnp.where(new_visible, new_scores, -1e30)
    row_max = jnp.maximum(jnp.max(old_scores, axis=-1), jnp.max(new_scores, axis=-1))[..., None]
    old_weights = jnp.where(old_visible, jnp.exp(old_scores - row_max), 0.0)
    new_weights = jnp.where(new_visible, jnp.exp(new_scores - row_max), 0.0)
    total = jnp.sum(old_weights, axis=-1) + jnp.sum(new_weights, axis=-1)
    summed = jnp.einsum(
        "hgtj,hjd->hgtd",
        old_weights.astype(jnp.bfloat16),
        old_values,
        preferred_element_type=jnp.float32,
    ) + jnp.einsum(
        "hgtu,hud->hgtd",
        new_weights.astype(jnp.bfloat16),
        fresh_values,
        preferred_element_type=jnp.float32,
    )
    result = (summed / total[..., None]).astype(jnp.bfloat16)
    return result.transpose(2, 0, 1, 3).reshape(query_rows, HQ * HD)


def solution(mesh):
    sizes = tuple(size for _, size in FSDP_PARTS)
    fine = jax.sharding.Mesh(
        mesh.devices.reshape(sizes + (mesh.shape["sp"],)), FSDP_AXES + ("sp",)
    )
    fsdp = FSDP_AXES
    placed = (
        P(fsdp, None),
        P(fsdp + ("sp",), None),
        P(fsdp, "sp"),
        P(fsdp, "sp"),
        P(fsdp, None, "sp"),
        P(fsdp, None, "sp"),
        P(fsdp),
        P(fsdp),
    )
    return jax.shard_map(
        per_device, mesh=fine, in_specs=placed, out_specs=P(fsdp + ("sp",), None), check_vma=False
    )
```

```python
import math

import jax
import jax.numpy as jnp
from jax import lax
from jax.sharding import PartitionSpec as P

HD = 128
HQ = 32
KVH = 4
YARN_SCALE = 16
ORIG_CTX = 8192


rope_base = 500000.0
beta_fast = 32.0
beta_slow = 1.0


def yarn_tables(positions, head_size):
    half_size = head_size // 2
    index_row = jnp.arange(half_size, dtype=jnp.float32)
    inverse = jnp.power(rope_base, -2.0 * index_row / head_size)
    wavelength = 2.0 * math.pi / inverse
    ratio = ORIG_CTX / wavelength
    ramp = jnp.clip((ratio - beta_slow) / (beta_fast - beta_slow), 0.0, 1.0)
    freq = inverse / YARN_SCALE * (1.0 - ramp) + inverse * ramp
    factor = 0.1 * math.log(YARN_SCALE) + 1.0
    angles = positions[:, None] * freq[None, :]
    return (jnp.cos(angles) * factor, jnp.sin(angles) * factor)


def rotate(values, cosine_table, sine_table, head_count):
    row_count = values.shape[0]
    half_size = cosine_table.shape[1]
    split = values.reshape(row_count, head_count, 2, half_size)
    first_half = split[:, :, 0]
    second_half = split[:, :, 1]
    cos_part = cosine_table[:, None, :]
    sin_part = sine_table[:, None, :]
    joined = jnp.stack(
        [
            first_half * cos_part - second_half * sin_part,
            second_half * cos_part + first_half * sin_part,
        ],
        axis=2,
    )
    return joined.reshape(row_count, head_count * 2 * half_size)


def attend_block(state, query_heads, key_block, value_block, visible):
    running_max, running_sum, weighted = state
    block_len = key_block.shape[0]
    kv_heads = query_heads.shape[0]
    key_heads = key_block.reshape(block_len, kv_heads, HD)
    value_heads = value_block.reshape(block_len, kv_heads, HD)
    scores = jnp.einsum(
        "hgqd,khd->hgqk", query_heads, key_heads, preferred_element_type=jnp.float32
    ) * HD ** (-0.5)
    scores = jnp.where(visible, scores, -1e30)
    new_max = jnp.maximum(running_max, jnp.max(scores, axis=-1))
    rescale = jnp.exp(running_max - new_max)
    weights = jnp.where(visible, jnp.exp(scores - new_max[..., None]), 0.0)
    running_sum = running_sum * rescale + jnp.sum(weights, axis=-1)
    product = jnp.einsum(
        "hgqk,khd->hgqd",
        weights.astype(jnp.bfloat16),
        value_heads,
        preferred_element_type=jnp.float32,
    )
    weighted = weighted * rescale[..., None] + product
    return (new_max, running_sum, weighted)


def attend_all(query_heads, old_keys, old_values, new_keys, new_values, live_count):
    kv_heads, group_size, query_rows, head_size = query_heads.shape
    slot_total = old_keys.shape[0]
    span_rows = new_keys.shape[0]
    state = (
        jnp.full((kv_heads, group_size, query_rows), -1e30, jnp.float32),
        jnp.zeros((kv_heads, group_size, query_rows), jnp.float32),
        jnp.zeros((kv_heads, group_size, query_rows, head_size), jnp.float32),
    )
    cache_block = min(256, slot_total)

    def cache_step(block_number, carried):
        start = block_number * cache_block
        slot_index = start + jnp.arange(cache_block, dtype=jnp.int32)
        visible = (slot_index >= slot_total - live_count)[None, None, None, :]
        return attend_block(carried, query_heads, old_keys, old_values, visible)

    state = lax.fori_loop(0, slot_total // cache_block, cache_step, state)
    new_block = min(256, span_rows)
    query_index = jnp.arange(query_rows, dtype=jnp.int32)

    def new_step(block_number, carried):
        start = block_number * new_block
        key_block = lax.dynamic_slice_in_dim(new_keys, start, new_block, 0)
        value_block = lax.dynamic_slice_in_dim(new_values, start, new_block, 0)
        key_index = start + jnp.arange(new_block, dtype=jnp.int32)
        visible = (key_index[None, :] <= query_index[:, None])[None, None, :, :]
        return attend_block(carried, query_heads, key_block, value_block, visible)

    state = lax.fori_loop(0, span_rows // new_block, new_step, state)
    running_max, running_sum, weighted = state
    result = (weighted / running_sum[..., None]).astype(jnp.bfloat16)
    return result.transpose(2, 0, 1, 3).reshape(query_rows, kv_heads * group_size * head_size)


FSDP_PARTS = (("ylo", 2), ("x", 4), ("z", 12), ("core", 2))
FSDP_AXES = tuple(name for name, _ in FSDP_PARTS)
GATHER_STAGES = (("ylo",), ("z",), ("x",), ("core",))


def gather_weights(shard):
    gathered = shard
    for stage in GATHER_STAGES[:-1]:
        gathered = lax.all_gather(gathered, stage, axis=0, tiled=False)
    early = [name for stage in reversed(GATHER_STAGES[:-1]) for name in stage]
    wanted = [name for name in FSDP_AXES if name in early]
    rank = len(early)
    gathered = gathered.transpose([early.index(name) for name in wanted] + [rank, rank + 1])
    (last,) = GATHER_STAGES[-1]
    gathered = lax.all_gather(gathered, last, axis=FSDP_AXES.index(last), tiled=False)
    return gathered.reshape(-1, shard.shape[1])


def gather_sp(block):
    count = lax.axis_size("sp")
    here = lax.axis_index("sp")
    pieces = [block]
    for shift in range(1, count):
        pairs = [(source, (source + shift) % count) for source in range(count)]
        pieces.append(lax.ppermute(block, "sp", perm=pairs))
    stacked = jnp.stack(pieces)
    order = (here - jnp.arange(count, dtype=jnp.int32)) % count
    return jnp.take(stacked, order, axis=0)


def exchange_causal(block, query_rows):
    count = lax.axis_size("sp")
    here = lax.axis_index("sp")
    split = block.shape[0] // 2
    head = block[:split]
    repeated = jnp.broadcast_to(head[None], (count,) + head.shape)
    head_all = lax.all_to_all(repeated, "sp", split_axis=0, concat_axis=0, tiled=True)
    tail = block[split:]
    readers = [j for j in range(count) if query_rows * (j + 1) > split]
    pieces = [tail]
    for shift in range(1, count):
        pairs = [((j - shift) % count, j) for j in readers]
        pieces.append(lax.ppermute(tail, "sp", perm=pairs))
    stacked = jnp.stack(pieces)
    order = (here - jnp.arange(count, dtype=jnp.int32)) % count
    tail_all = jnp.take(stacked, order, axis=0)
    return jnp.concatenate([head_all, tail_all], axis=1)


def per_device(
    hidden_rows, queries, key_weight, value_weight, cache_keys, cache_values, span_index, prefix_len
):
    span_rows = hidden_rows.shape[0]
    model_width = hidden_rows.shape[1]
    query_rows = queries.shape[0]
    kv_cols = key_weight.shape[1]
    kv_local = kv_cols // HD
    group_size = HQ // KVH
    slot_total = cache_keys.shape[1]
    sp_index = lax.axis_index("sp")
    block_start = span_index[0] * span_rows
    positions = (block_start + jnp.arange(span_rows, dtype=jnp.int32)).astype(jnp.float32)
    cosine_table, sine_table = yarn_tables(positions, HD)
    first_query = sp_index * query_rows
    query_positions = (
        block_start + first_query + jnp.arange(query_rows, dtype=jnp.int32)
    ).astype(jnp.float32)
    query_cosine, query_sine = yarn_tables(query_positions, HD)
    live_count = prefix_len[0]

    cache_kv = jnp.concatenate([cache_keys[0], cache_values[0]], axis=1)
    cache_all = gather_sp(cache_kv)

    whole_kv = gather_weights(jnp.concatenate([key_weight, value_weight], axis=1))
    kv_sum = jnp.dot(hidden_rows, whole_kv[:model_width], preferred_element_type=jnp.float32)
    new_keys = rotate(kv_sum[:, :kv_cols], cosine_table, sine_table, kv_local).astype(jnp.bfloat16)
    new_values = kv_sum[:, kv_cols:].astype(jnp.bfloat16)
    new_kv = jnp.concatenate([new_keys, new_values], axis=1)
    new_all = exchange_causal(new_kv, query_rows)

    rotated_q = rotate(queries.astype(jnp.float32), query_cosine, query_sine, HQ).astype(
        jnp.bfloat16
    )
    query_heads = rotated_q.reshape(query_rows, KVH, group_size, HD)
    scale = HD ** (-0.5)
    old_keys = cache_all[:, :, :HD]
    old_values = cache_all[:, :, HD:]
    fresh_keys = new_all[:, :, :HD]
    fresh_values = new_all[:, :, HD:]
    old_scores = jnp.einsum(
        "thgd,hjd->hgtj", query_heads, old_keys, preferred_element_type=jnp.float32
    ) * scale
    new_scores = jnp.einsum(
        "thgd,hud->hgtu", query_heads, fresh_keys, preferred_element_type=jnp.float32
    ) * scale
    slot_index = jnp.arange(slot_total, dtype=jnp.int32)
    old_visible = (slot_index >= slot_total - live_count)[None, None, None, :]
    key_index = jnp.arange(span_rows, dtype=jnp.int32)
    query_index = first_query + jnp.arange(query_rows, dtype=jnp.int32)
    new_visible = (key_index[None, :] <= query_index[:, None])[None, None, :, :]
    old_scores = jnp.where(old_visible, old_scores, -1e30)
    new_scores = jnp.where(new_visible, new_scores, -1e30)
    row_max = jnp.maximum(jnp.max(old_scores, axis=-1), jnp.max(new_scores, axis=-1))[..., None]
    old_weights = jnp.where(old_visible, jnp.exp(old_scores - row_max), 0.0)
    new_weights = jnp.where(new_visible, jnp.exp(new_scores - row_max), 0.0)
    total = jnp.sum(old_weights, axis=-1) + jnp.sum(new_weights, axis=-1)
    summed = jnp.einsum(
        "hgtj,hjd->hgtd",
        old_weights.astype(jnp.bfloat16),
        old_values,
        preferred_element_type=jnp.float32,
    ) + jnp.einsum(
        "hgtu,hud->hgtd",
        new_weights.astype(jnp.bfloat16),
        fresh_values,
        preferred_element_type=jnp.float32,
    )
    result = (summed / total[..., None]).astype(jnp.bfloat16)
    return result.transpose(2, 0, 1, 3).reshape(query_rows, HQ * HD)


def solution(mesh):
    sizes = tuple(size for _, size in FSDP_PARTS)
    fine = jax.sharding.Mesh(
        mesh.devices.reshape(sizes + (mesh.shape["sp"],)), FSDP_AXES + ("sp",)
    )
    fsdp = FSDP_AXES
    placed = (
        P(fsdp, None),
        P(fsdp + ("sp",), None),
        P(fsdp, "sp"),
        P(fsdp, "sp"),
        P(fsdp, None, "sp"),
        P(fsdp, None, "sp"),
        P(fsdp),
        P(fsdp),
    )
    return jax.shard_map(
        per_device, mesh=fine, in_specs=placed, out_specs=P(fsdp + ("sp",), None), check_vma=False
    )
```

```python
import math

import jax
import jax.numpy as jnp
from jax import lax
from jax.sharding import PartitionSpec as P

HD = 128
HQ = 32
KVH = 4
YARN_SCALE = 16
ORIG_CTX = 8192


rope_base = 500000.0
beta_fast = 32.0
beta_slow = 1.0


def yarn_tables(positions, head_size):
    half_size = head_size // 2
    index_row = jnp.arange(half_size, dtype=jnp.float32)
    inverse = jnp.power(rope_base, -2.0 * index_row / head_size)
    wavelength = 2.0 * math.pi / inverse
    ratio = ORIG_CTX / wavelength
    ramp = jnp.clip((ratio - beta_slow) / (beta_fast - beta_slow), 0.0, 1.0)
    freq = inverse / YARN_SCALE * (1.0 - ramp) + inverse * ramp
    factor = 0.1 * math.log(YARN_SCALE) + 1.0
    angles = positions[:, None] * freq[None, :]
    return (jnp.cos(angles) * factor, jnp.sin(angles) * factor)


def rotate(values, cosine_table, sine_table, head_count):
    row_count = values.shape[0]
    half_size = cosine_table.shape[1]
    split = values.reshape(row_count, head_count, 2, half_size)
    first_half = split[:, :, 0]
    second_half = split[:, :, 1]
    cos_part = cosine_table[:, None, :]
    sin_part = sine_table[:, None, :]
    joined = jnp.stack(
        [
            first_half * cos_part - second_half * sin_part,
            second_half * cos_part + first_half * sin_part,
        ],
        axis=2,
    )
    return joined.reshape(row_count, head_count * 2 * half_size)


def attend_block(state, query_heads, key_block, value_block, visible):
    running_max, running_sum, weighted = state
    block_len = key_block.shape[0]
    kv_heads = query_heads.shape[0]
    key_heads = key_block.reshape(block_len, kv_heads, HD)
    value_heads = value_block.reshape(block_len, kv_heads, HD)
    scores = jnp.einsum(
        "hgqd,khd->hgqk", query_heads, key_heads, preferred_element_type=jnp.float32
    ) * HD ** (-0.5)
    scores = jnp.where(visible, scores, -1e30)
    new_max = jnp.maximum(running_max, jnp.max(scores, axis=-1))
    rescale = jnp.exp(running_max - new_max)
    weights = jnp.where(visible, jnp.exp(scores - new_max[..., None]), 0.0)
    running_sum = running_sum * rescale + jnp.sum(weights, axis=-1)
    product = jnp.einsum(
        "hgqk,khd->hgqd",
        weights.astype(jnp.bfloat16),
        value_heads,
        preferred_element_type=jnp.float32,
    )
    weighted = weighted * rescale[..., None] + product
    return (new_max, running_sum, weighted)


def attend_all(query_heads, old_keys, old_values, new_keys, new_values, live_count):
    kv_heads, group_size, query_rows, head_size = query_heads.shape
    slot_total = old_keys.shape[0]
    span_rows = new_keys.shape[0]
    state = (
        jnp.full((kv_heads, group_size, query_rows), -1e30, jnp.float32),
        jnp.zeros((kv_heads, group_size, query_rows), jnp.float32),
        jnp.zeros((kv_heads, group_size, query_rows, head_size), jnp.float32),
    )
    cache_block = min(256, slot_total)

    def cache_step(block_number, carried):
        start = block_number * cache_block
        slot_index = start + jnp.arange(cache_block, dtype=jnp.int32)
        visible = (slot_index >= slot_total - live_count)[None, None, None, :]
        return attend_block(carried, query_heads, old_keys, old_values, visible)

    state = lax.fori_loop(0, slot_total // cache_block, cache_step, state)
    new_block = min(256, span_rows)
    query_index = jnp.arange(query_rows, dtype=jnp.int32)

    def new_step(block_number, carried):
        start = block_number * new_block
        key_block = lax.dynamic_slice_in_dim(new_keys, start, new_block, 0)
        value_block = lax.dynamic_slice_in_dim(new_values, start, new_block, 0)
        key_index = start + jnp.arange(new_block, dtype=jnp.int32)
        visible = (key_index[None, :] <= query_index[:, None])[None, None, :, :]
        return attend_block(carried, query_heads, key_block, value_block, visible)

    state = lax.fori_loop(0, span_rows // new_block, new_step, state)
    running_max, running_sum, weighted = state
    result = (weighted / running_sum[..., None]).astype(jnp.bfloat16)
    return result.transpose(2, 0, 1, 3).reshape(query_rows, kv_heads * group_size * head_size)


FSDP_PARTS = (("ylo", 2), ("x", 4), ("z", 12), ("core", 2))
FSDP_AXES = tuple(name for name, _ in FSDP_PARTS)
GATHER_STAGES = (("z",), ("ylo",), ("x",), ("core",))


def gather_weights(shard):
    gathered = shard
    for stage in GATHER_STAGES[:-1]:
        gathered = lax.all_gather(gathered, stage, axis=0, tiled=False)
    early = [name for stage in reversed(GATHER_STAGES[:-1]) for name in stage]
    wanted = [name for name in FSDP_AXES if name in early]
    rank = len(early)
    gathered = gathered.transpose([early.index(name) for name in wanted] + [rank, rank + 1])
    (last,) = GATHER_STAGES[-1]
    gathered = lax.all_gather(gathered, last, axis=FSDP_AXES.index(last), tiled=False)
    return gathered.reshape(-1, shard.shape[1])


def gather_sp(block):
    count = lax.axis_size("sp")
    here = lax.axis_index("sp")
    pieces = [block]
    for shift in range(1, count):
        pairs = [(source, (source + shift) % count) for source in range(count)]
        pieces.append(lax.ppermute(block, "sp", perm=pairs))
    stacked = jnp.stack(pieces)
    order = (here - jnp.arange(count, dtype=jnp.int32)) % count
    return jnp.take(stacked, order, axis=0)


def exchange_causal(block, query_rows):
    count = lax.axis_size("sp")
    here = lax.axis_index("sp")
    split = block.shape[0] // 2
    head = block[:split]
    repeated = jnp.broadcast_to(head[None], (count,) + head.shape)
    head_all = lax.all_to_all(repeated, "sp", split_axis=0, concat_axis=0, tiled=True)
    tail = block[split:]
    readers = [j for j in range(count) if query_rows * (j + 1) > split]
    pieces = [tail]
    for shift in range(1, count):
        pairs = [((j - shift) % count, j) for j in readers]
        pieces.append(lax.ppermute(tail, "sp", perm=pairs))
    stacked = jnp.stack(pieces)
    order = (here - jnp.arange(count, dtype=jnp.int32)) % count
    tail_all = jnp.take(stacked, order, axis=0)
    return jnp.concatenate([head_all, tail_all], axis=1)


def per_device(
    hidden_rows, queries, key_weight, value_weight, cache_keys, cache_values, span_index, prefix_len
):
    span_rows = hidden_rows.shape[0]
    model_width = hidden_rows.shape[1]
    query_rows = queries.shape[0]
    kv_cols = key_weight.shape[1]
    kv_local = kv_cols // HD
    group_size = HQ // KVH
    slot_total = cache_keys.shape[1]
    sp_index = lax.axis_index("sp")
    block_start = span_index[0] * span_rows
    positions = (block_start + jnp.arange(span_rows, dtype=jnp.int32)).astype(jnp.float32)
    cosine_table, sine_table = yarn_tables(positions, HD)
    first_query = sp_index * query_rows
    query_positions = (
        block_start + first_query + jnp.arange(query_rows, dtype=jnp.int32)
    ).astype(jnp.float32)
    query_cosine, query_sine = yarn_tables(query_positions, HD)
    live_count = prefix_len[0]

    cache_kv = jnp.concatenate([cache_keys[0], cache_values[0]], axis=1)
    cache_all = gather_sp(cache_kv)

    whole_kv = gather_weights(jnp.concatenate([key_weight, value_weight], axis=1))
    kv_sum = jnp.dot(hidden_rows, whole_kv[:model_width], preferred_element_type=jnp.float32)
    new_keys = rotate(kv_sum[:, :kv_cols], cosine_table, sine_table, kv_local).astype(jnp.bfloat16)
    new_values = kv_sum[:, kv_cols:].astype(jnp.bfloat16)
    new_kv = jnp.concatenate([new_keys, new_values], axis=1)
    new_all = exchange_causal(new_kv, query_rows)

    rotated_q = rotate(queries.astype(jnp.float32), query_cosine, query_sine, HQ).astype(
        jnp.bfloat16
    )
    query_heads = rotated_q.reshape(query_rows, KVH, group_size, HD)
    scale = HD ** (-0.5)
    old_keys = cache_all[:, :, :HD]
    old_values = cache_all[:, :, HD:]
    fresh_keys = new_all[:, :, :HD]
    fresh_values = new_all[:, :, HD:]
    old_scores = jnp.einsum(
        "thgd,hjd->hgtj", query_heads, old_keys, preferred_element_type=jnp.float32
    ) * scale
    new_scores = jnp.einsum(
        "thgd,hud->hgtu", query_heads, fresh_keys, preferred_element_type=jnp.float32
    ) * scale
    slot_index = jnp.arange(slot_total, dtype=jnp.int32)
    old_visible = (slot_index >= slot_total - live_count)[None, None, None, :]
    key_index = jnp.arange(span_rows, dtype=jnp.int32)
    query_index = first_query + jnp.arange(query_rows, dtype=jnp.int32)
    new_visible = (key_index[None, :] <= query_index[:, None])[None, None, :, :]
    old_scores = jnp.where(old_visible, old_scores, -1e30)
    new_scores = jnp.where(new_visible, new_scores, -1e30)
    row_max = jnp.maximum(jnp.max(old_scores, axis=-1), jnp.max(new_scores, axis=-1))[..., None]
    old_weights = jnp.where(old_visible, jnp.exp(old_scores - row_max), 0.0)
    new_weights = jnp.where(new_visible, jnp.exp(new_scores - row_max), 0.0)
    total = jnp.sum(old_weights, axis=-1) + jnp.sum(new_weights, axis=-1)
    summed = jnp.einsum(
        "hgtj,hjd->hgtd",
        old_weights.astype(jnp.bfloat16),
        old_values,
        preferred_element_type=jnp.float32,
    ) + jnp.einsum(
        "hgtu,hud->hgtd",
        new_weights.astype(jnp.bfloat16),
        fresh_values,
        preferred_element_type=jnp.float32,
    )
    result = (summed / total[..., None]).astype(jnp.bfloat16)
    return result.transpose(2, 0, 1, 3).reshape(query_rows, HQ * HD)


def solution(mesh):
    sizes = tuple(size for _, size in FSDP_PARTS)
    fine = jax.sharding.Mesh(
        mesh.devices.reshape(sizes + (mesh.shape["sp"],)), FSDP_AXES + ("sp",)
    )
    fsdp = FSDP_AXES
    placed = (
        P(fsdp, None),
        P(fsdp + ("sp",), None),
        P(fsdp, "sp"),
        P(fsdp, "sp"),
        P(fsdp, None, "sp"),
        P(fsdp, None, "sp"),
        P(fsdp),
        P(fsdp),
    )
    return jax.shard_map(
        per_device, mesh=fine, in_specs=placed, out_specs=P(fsdp + ("sp",), None), check_vma=False
    )
```

```python
import math

import jax
import jax.numpy as jnp
from jax import lax
from jax.sharding import PartitionSpec as P

HD = 128
HQ = 32
KVH = 4
YARN_SCALE = 16
ORIG_CTX = 8192


rope_base = 500000.0
beta_fast = 32.0
beta_slow = 1.0


def yarn_tables(positions, head_size):
    half_size = head_size // 2
    index_row = jnp.arange(half_size, dtype=jnp.float32)
    inverse = jnp.power(rope_base, -2.0 * index_row / head_size)
    wavelength = 2.0 * math.pi / inverse
    ratio = ORIG_CTX / wavelength
    ramp = jnp.clip((ratio - beta_slow) / (beta_fast - beta_slow), 0.0, 1.0)
    freq = inverse / YARN_SCALE * (1.0 - ramp) + inverse * ramp
    factor = 0.1 * math.log(YARN_SCALE) + 1.0
    angles = positions[:, None] * freq[None, :]
    return (jnp.cos(angles) * factor, jnp.sin(angles) * factor)


def rotate(values, cosine_table, sine_table, head_count):
    row_count = values.shape[0]
    half_size = cosine_table.shape[1]
    split = values.reshape(row_count, head_count, 2, half_size)
    first_half = split[:, :, 0]
    second_half = split[:, :, 1]
    cos_part = cosine_table[:, None, :]
    sin_part = sine_table[:, None, :]
    joined = jnp.stack(
        [
            first_half * cos_part - second_half * sin_part,
            second_half * cos_part + first_half * sin_part,
        ],
        axis=2,
    )
    return joined.reshape(row_count, head_count * 2 * half_size)


def attend_block(state, query_heads, key_block, value_block, visible):
    running_max, running_sum, weighted = state
    block_len = key_block.shape[0]
    kv_heads = query_heads.shape[0]
    key_heads = key_block.reshape(block_len, kv_heads, HD)
    value_heads = value_block.reshape(block_len, kv_heads, HD)
    scores = jnp.einsum(
        "hgqd,khd->hgqk", query_heads, key_heads, preferred_element_type=jnp.float32
    ) * HD ** (-0.5)
    scores = jnp.where(visible, scores, -1e30)
    new_max = jnp.maximum(running_max, jnp.max(scores, axis=-1))
    rescale = jnp.exp(running_max - new_max)
    weights = jnp.where(visible, jnp.exp(scores - new_max[..., None]), 0.0)
    running_sum = running_sum * rescale + jnp.sum(weights, axis=-1)
    product = jnp.einsum(
        "hgqk,khd->hgqd",
        weights.astype(jnp.bfloat16),
        value_heads,
        preferred_element_type=jnp.float32,
    )
    weighted = weighted * rescale[..., None] + product
    return (new_max, running_sum, weighted)


def attend_all(query_heads, old_keys, old_values, new_keys, new_values, live_count):
    kv_heads, group_size, query_rows, head_size = query_heads.shape
    slot_total = old_keys.shape[0]
    span_rows = new_keys.shape[0]
    state = (
        jnp.full((kv_heads, group_size, query_rows), -1e30, jnp.float32),
        jnp.zeros((kv_heads, group_size, query_rows), jnp.float32),
        jnp.zeros((kv_heads, group_size, query_rows, head_size), jnp.float32),
    )
    cache_block = min(256, slot_total)

    def cache_step(block_number, carried):
        start = block_number * cache_block
        slot_index = start + jnp.arange(cache_block, dtype=jnp.int32)
        visible = (slot_index >= slot_total - live_count)[None, None, None, :]
        return attend_block(carried, query_heads, old_keys, old_values, visible)

    state = lax.fori_loop(0, slot_total // cache_block, cache_step, state)
    new_block = min(256, span_rows)
    query_index = jnp.arange(query_rows, dtype=jnp.int32)

    def new_step(block_number, carried):
        start = block_number * new_block
        key_block = lax.dynamic_slice_in_dim(new_keys, start, new_block, 0)
        value_block = lax.dynamic_slice_in_dim(new_values, start, new_block, 0)
        key_index = start + jnp.arange(new_block, dtype=jnp.int32)
        visible = (key_index[None, :] <= query_index[:, None])[None, None, :, :]
        return attend_block(carried, query_heads, key_block, value_block, visible)

    state = lax.fori_loop(0, span_rows // new_block, new_step, state)
    running_max, running_sum, weighted = state
    result = (weighted / running_sum[..., None]).astype(jnp.bfloat16)
    return result.transpose(2, 0, 1, 3).reshape(query_rows, kv_heads * group_size * head_size)


FSDP_PARTS = (("ylo", 2), ("x", 4), ("z", 12), ("core", 2))
FSDP_AXES = tuple(name for name, _ in FSDP_PARTS)
GATHER_STAGES = (("ylo",), ("z",), ("x",), ("core",))


def gather_weights(shard):
    gathered = shard
    for stage in GATHER_STAGES:
        gathered = lax.all_gather(gathered, stage, axis=0, tiled=False)
        if len(stage) > 1:
            sizes = tuple(dict(FSDP_PARTS)[name] for name in stage)
            gathered = gathered.reshape(sizes + gathered.shape[1:])
    layout = []
    for stage in reversed(GATHER_STAGES):
        layout.extend(stage)
    perm = [layout.index(name) for name in FSDP_AXES]
    rank = len(FSDP_AXES)
    gathered = gathered.transpose(perm + [rank, rank + 1])
    return gathered.reshape(-1, shard.shape[1])


def gather_sp(block):
    count = lax.axis_size("sp")
    here = lax.axis_index("sp")
    pieces = [block]
    for shift in range(1, count):
        pairs = [(source, (source + shift) % count) for source in range(count)]
        pieces.append(lax.ppermute(block, "sp", perm=pairs))
    stacked = jnp.stack(pieces)
    order = (here - jnp.arange(count, dtype=jnp.int32)) % count
    return jnp.take(stacked, order, axis=0)


def exchange_causal(block, query_rows):
    count = lax.axis_size("sp")
    here = lax.axis_index("sp")
    split = block.shape[0] // 2
    head = block[:split]
    repeated = jnp.broadcast_to(head[None], (count,) + head.shape)
    head_all = lax.all_to_all(repeated, "sp", split_axis=0, concat_axis=0, tiled=True)
    tail = block[split:]
    readers = [j for j in range(count) if query_rows * (j + 1) > split]
    pieces = [tail]
    for shift in range(1, count):
        pairs = [((j - shift) % count, j) for j in readers]
        pieces.append(lax.ppermute(tail, "sp", perm=pairs))
    stacked = jnp.stack(pieces)
    order = (here - jnp.arange(count, dtype=jnp.int32)) % count
    tail_all = jnp.take(stacked, order, axis=0)
    return jnp.concatenate([head_all, tail_all], axis=1)


def per_device(
    hidden_rows, queries, key_weight, value_weight, cache_keys, cache_values, span_index, prefix_len
):
    span_rows = hidden_rows.shape[0]
    model_width = hidden_rows.shape[1]
    query_rows = queries.shape[0]
    kv_cols = key_weight.shape[1]
    kv_local = kv_cols // HD
    group_size = HQ // KVH
    slot_total = cache_keys.shape[1]
    sp_index = lax.axis_index("sp")
    block_start = span_index[0] * span_rows
    positions = (block_start + jnp.arange(span_rows, dtype=jnp.int32)).astype(jnp.float32)
    cosine_table, sine_table = yarn_tables(positions, HD)
    first_query = sp_index * query_rows
    query_positions = (
        block_start + first_query + jnp.arange(query_rows, dtype=jnp.int32)
    ).astype(jnp.float32)
    query_cosine, query_sine = yarn_tables(query_positions, HD)
    live_count = prefix_len[0]

    cache_kv = jnp.concatenate([cache_keys[0], cache_values[0]], axis=1)
    cache_all = gather_sp(cache_kv)

    whole_kv = gather_weights(jnp.concatenate([key_weight, value_weight], axis=1))
    kv_sum = jnp.dot(hidden_rows, whole_kv[:model_width], preferred_element_type=jnp.float32)
    new_keys = rotate(kv_sum[:, :kv_cols], cosine_table, sine_table, kv_local).astype(jnp.bfloat16)
    new_values = kv_sum[:, kv_cols:].astype(jnp.bfloat16)
    new_kv = jnp.concatenate([new_keys, new_values], axis=1)
    new_all = exchange_causal(new_kv, query_rows)

    rotated_q = rotate(queries.astype(jnp.float32), query_cosine, query_sine, HQ).astype(
        jnp.bfloat16
    )
    query_heads = rotated_q.reshape(query_rows, KVH, group_size, HD)
    scale = HD ** (-0.5)
    old_keys = cache_all[:, :, :HD]
    old_values = cache_all[:, :, HD:]
    fresh_keys = new_all[:, :, :HD]
    fresh_values = new_all[:, :, HD:]
    old_scores = jnp.einsum(
        "thgd,hjd->hgtj", query_heads, old_keys, preferred_element_type=jnp.float32
    ) * scale
    new_scores = jnp.einsum(
        "thgd,hud->hgtu", query_heads, fresh_keys, preferred_element_type=jnp.float32
    ) * scale
    slot_index = jnp.arange(slot_total, dtype=jnp.int32)
    old_visible = (slot_index >= slot_total - live_count)[None, None, None, :]
    key_index = jnp.arange(span_rows, dtype=jnp.int32)
    query_index = first_query + jnp.arange(query_rows, dtype=jnp.int32)
    new_visible = (key_index[None, :] <= query_index[:, None])[None, None, :, :]
    old_scores = jnp.where(old_visible, old_scores, -1e30)
    new_scores = jnp.where(new_visible, new_scores, -1e30)
    row_max = jnp.maximum(jnp.max(old_scores, axis=-1), jnp.max(new_scores, axis=-1))[..., None]
    old_weights = jnp.where(old_visible, jnp.exp(old_scores - row_max), 0.0)
    new_weights = jnp.where(new_visible, jnp.exp(new_scores - row_max), 0.0)
    total = jnp.sum(old_weights, axis=-1) + jnp.sum(new_weights, axis=-1)
    summed = jnp.einsum(
        "hgtj,hjd->hgtd",
        old_weights.astype(jnp.bfloat16),
        old_values,
        preferred_element_type=jnp.float32,
    ) + jnp.einsum(
        "hgtu,hud->hgtd",
        new_weights.astype(jnp.bfloat16),
        fresh_values,
        preferred_element_type=jnp.float32,
    )
    result = (summed / total[..., None]).astype(jnp.bfloat16)
    return result.transpose(2, 0, 1, 3).reshape(query_rows, HQ * HD)


def solution(mesh):
    sizes = tuple(size for _, size in FSDP_PARTS)
    fine = jax.sharding.Mesh(
        mesh.devices.reshape(sizes + (mesh.shape["sp"],)), FSDP_AXES + ("sp",)
    )
    fsdp = FSDP_AXES
    placed = (
        P(fsdp, None),
        P(fsdp + ("sp",), None),
        P(fsdp, "sp"),
        P(fsdp, "sp"),
        P(fsdp, None, "sp"),
        P(fsdp, None, "sp"),
        P(fsdp),
        P(fsdp),
    )
    return jax.shard_map(
        per_device, mesh=fine, in_specs=placed, out_specs=P(fsdp + ("sp",), None), check_vma=False
    )
```
